512 devices in a mesh: seq: 8 (over z_lo, core), ctx: 64 (over z_hi, y, x).
Axes of the slice: x: 4, y: 8, z: 8 (z_hi: 2, z_lo: 4; z = z_hi * 4 + z_lo), core: 2. Of those that a mesh axis runs over, the one named last changes fastest.
Arguments:
- tokens: bfloat16 [8, 8192, 2048], P('seq', 'ctx'), may hold values from -80 to 80
- qkv_weight: bfloat16 [2048, 1536], P(None, 'seq'), may hold values from -0.125 to 0.125
- doc_lengths: int32 [8, 36], P('seq'), may hold values from 1 to 1024, 8192 in all within a row
- span_order: int32 [8, 128], P('seq'), may hold values from 0 to 127, as said below
Outputs:
- attended: bfloat16 [8, 8192, 1024], P('seq', 'ctx')
The draws below stay inside these ranges and needn't reach their ends.
Inputs may be any that keep to these rules, and one draw needn't show every extreme that they name: `doc_lengths`: each row sums to 8192; its largest entry is exactly 1024. `span_order`: in each row, slots 2 i and 2 i + 1 hold spans i and 127 - i, in an order drawn for each pair.
All inputs are finite; a program needn't handle non-finite values.
Results may differ from the reference program's by a relative error of at most 0.012.
The reference program's roundings to bfloat16 on the way count: a program that leaves them out, or rounds other values in their place, can miss the bound.
Values may be sent and summed in bfloat16 or wider, within the bound.
No kernel may reach another device: no remote copies, remote signals or barrier semaphores. Data moves between devices by JAX's collectives and lax.ppermute only.
A program may use at most 192 MiB of HBM per device.

```python
import math
import jax
import jax.numpy as jnp
import numpy as np
from jax import lax

D = 2048
QUERY_HEADS = 16
KEY_VALUE_HEADS = 4
HEAD_SIZE = 64
QUERY_PER_KV = 4
QKV = 1536
SPAN = 64
SEQS = 8
LEN = 8192
SPANS = 128
DOC_MOST = 1024
DOCS = 36


def draw_tokens(key, part):
    first = jax.random.fold_in(key, 0)
    value_rows = jax.random.normal(first, (SEQS, LEN, D), jnp.float32)
    return jnp.clip(value_rows, -80.0, 80.0).astype(jnp.bfloat16)


def draw_span_order(key, part):
    pairs = SPANS // 2
    flips = jax.random.randint(jax.random.fold_in(key, 7), (SEQS, pairs), 0, 2).astype(jnp.int32)
    early = jnp.broadcast_to(jnp.arange(pairs, dtype=jnp.int32)[None, :], (SEQS, pairs))
    late = (SPANS - 1 - early).astype(jnp.int32)
    first_slot = jnp.where(flips == 1, late, early)
    second_slot = jnp.where(flips == 1, early, late)
    return jnp.stack([first_slot, second_slot], axis=-1).reshape(SEQS, SPANS).astype(jnp.int32)


def steps_of(key, extent, shards, low, largest):
    def one(axis_at, blocks):
        steps = jax.random.uniform(jax.random.fold_in(jax.random.fold_in(key, 6), axis_at), (blocks,), jnp.float32, low / len(shards), largest / len(shards))
        return jnp.repeat(jnp.exp(steps), extent[axis_at] // blocks).reshape((-1,) + (1,) * (len(extent) - axis_at - 1))

    gain = one(*shards[0])
    for cut in shards[1:]:
        gain = gain * one(*cut)
    return gain


def length_profile(number_of, total, limit, skew):
    portions = [(1 << 20) // math.isqrt(grade ** skew) + 1 for grade in range(2, number_of + 1)]
    rest, holding = total - limit - (number_of - 1), [1] * (number_of - 1)
    while rest > 0:
        free = [i for i in range(number_of - 1) if holding[i] < limit]
        pool, budget = sum([portions[i] for i in free]), rest
        for i in free:
            extra = min(limit - holding[i], max(1, budget * portions[i] // pool), rest)
            holding[i] = holding[i] + extra
            rest = rest - extra
    return np.array([limit] + holding)


def uneven_parts(own_key, count, total, most, slope):
    if count == 2:
        one = jax.random.randint(own_key, (), max(1, total - most), min(most, total - 1) + 1)
        return jnp.stack([one, total - one])
    lengths = jnp.asarray(length_profile(count, total, most, slope), jnp.int32)
    pairs = (count - 1) // 2
    donor, receiver = lengths[1:1 + 2 * pairs:2], lengths[2:2 + 2 * pairs:2]
    margin = jnp.minimum(donor - 1, most - receiver)
    passed = jax.random.randint(jax.random.fold_in(own_key, 1), (pairs,), 0, 1 << 20) % (margin + 1)
    lengths = lengths.at[1:1 + 2 * pairs:2].set(donor - passed).at[2:2 + 2 * pairs:2].set(receiver + passed)
    return lengths[jax.random.permutation(jax.random.fold_in(own_key, 2), count)]


def normal_values(rng, shape, deviation, limit, pieces=(), held_as=jnp.bfloat16):
    values = jax.random.normal(rng, shape, jnp.float32) * deviation
    if len(pieces) > 0:
        values = steps_of(rng, shape, pieces, -0.22, 0.18) * values
    return jnp.clip(values, min=-limit, max=limit).astype(held_as)


def setup_inputs(seed: int = 0) -> dict:
    splits = jax.random.split(jax.random.key(seed), 5)
    return {
        "tokens": draw_tokens(jax.random.fold_in(splits[4], 71), 0),
        "qkv_weight": normal_values(splits[1], (D, QKV), D ** -0.5, 0.125, ((1, 8),)),
        "doc_lengths": jax.vmap(lambda own: uneven_parts(own, DOCS, LEN, DOC_MOST, 2))(jax.random.split(splits[2], SEQS)).reshape((SEQS, DOCS)).astype(jnp.int32),
        "span_order": draw_span_order(jax.random.fold_in(splits[4], 71), 0),
    }


def apply_rotary(value_rows, token_positions):
    token_count = value_rows.shape[0]
    heads = value_rows.reshape(token_count, -1, HEAD_SIZE)
    half = HEAD_SIZE // 2
    freq = 500000.0 ** (-jnp.arange(half, dtype=jnp.float32) * 2.0 / HEAD_SIZE)
    angle = token_positions.astype(jnp.float32)[:, None] * freq[None, :]
    cosine = jnp.cos(angle)[:, None, :]
    sine = jnp.sin(angle)[:, None, :]
    first = heads[..., :half]
    second = heads[..., half:]
    turned = jnp.concatenate([first * cosine - second * sine, second * cosine + first * sine], axis=-1)
    return turned.reshape(token_count, -1)


def positions(order_row):
    offsets = jnp.arange(SPAN, dtype=jnp.int32)
    return (order_row[:, None] * SPAN + offsets[None, :]).reshape(-1).astype(jnp.int32)


def documents(lengths_row, token_positions):
    ends = jnp.cumsum(lengths_row).astype(jnp.int32)
    return jnp.sum((ends[None, :] <= token_positions[:, None]).astype(jnp.int32), axis=1)


def one_sequence(rows, lengths_row, order_row, qkv_weight):
    token_positions = positions(order_row)
    docs = documents(lengths_row, token_positions)
    query_key_value = jnp.dot(rows, qkv_weight, preferred_element_type=jnp.float32).astype(jnp.bfloat16)
    query_rows = apply_rotary(query_key_value[:, :QUERY_HEADS * HEAD_SIZE].astype(jnp.float32), token_positions).astype(jnp.bfloat16)
    key_rows = apply_rotary(query_key_value[:, QUERY_HEADS * HEAD_SIZE:(QUERY_HEADS + KEY_VALUE_HEADS) * HEAD_SIZE].astype(jnp.float32), token_positions).astype(jnp.bfloat16)
    value_rows = query_key_value[:, (QUERY_HEADS + KEY_VALUE_HEADS) * HEAD_SIZE:]
    live = (docs[:, None] == docs[None, :]) & (token_positions[None, :] <= token_positions[:, None])

    def one_head(head):
        group = head // QUERY_PER_KV
        query_h = lax.dynamic_slice_in_dim(query_rows, head * HEAD_SIZE, HEAD_SIZE, 1)
        key_h = lax.dynamic_slice_in_dim(key_rows, group * HEAD_SIZE, HEAD_SIZE, 1)
        value_h = lax.dynamic_slice_in_dim(value_rows, group * HEAD_SIZE, HEAD_SIZE, 1)
        scores = jnp.dot(query_h, key_h.T, preferred_element_type=jnp.float32) * 0.125
        scores = jnp.where(live, scores, -1e30)
        top = jnp.max(scores, axis=1, keepdims=True)
        weights = jnp.where(live, jnp.exp(scores - top), 0.0)
        total = jnp.sum(weights, axis=1, keepdims=True)
        summed = jnp.dot(weights.astype(jnp.bfloat16), value_h, preferred_element_type=jnp.float32)
        return summed / total

    outputs = lax.map(one_head, jnp.arange(QUERY_HEADS, dtype=jnp.int32))
    return jnp.transpose(outputs, (1, 0, 2)).reshape(LEN, QUERY_HEADS * HEAD_SIZE).astype(jnp.bfloat16)


def reference(tokens, qkv_weight, doc_lengths, span_order):
    results = []
    for index in range(SEQS):
        results.append(one_sequence(tokens[index], doc_lengths[index], span_order[index], qkv_weight))
    return jnp.stack(results, axis=0)
```

```python
import jax
import jax.numpy as jnp
from jax import lax
from jax.sharding import PartitionSpec as P

QUERY_HEADS = 16
KEY_VALUE_HEADS = 4
HEAD_SIZE = 64
QUERY_PER_KV = 4
SPAN = 64
DOC_MOST = 1024
WINDOW = DOC_MOST // SPAN


def apply_rotary(value_rows, token_positions):
    token_count = value_rows.shape[0]
    heads = value_rows.reshape(token_count, -1, HEAD_SIZE)
    half = HEAD_SIZE // 2
    freq = 500000.0 ** (-jnp.arange(half, dtype=jnp.float32) * 2.0 / HEAD_SIZE)
    angle = token_positions.astype(jnp.float32)[:, None] * freq[None, :]
    cosine = jnp.cos(angle)[:, None, :]
    sine = jnp.sin(angle)[:, None, :]
    first = heads[..., :half]
    second = heads[..., half:]
    turned = jnp.concatenate(
        [first * cosine - second * sine, second * cosine + first * sine], axis=-1
    )
    return turned.reshape(token_count, -1)


def positions(order_row):
    offsets = jnp.arange(SPAN, dtype=jnp.int32)
    return (order_row[:, None] * SPAN + offsets[None, :]).reshape(-1)


def documents(lengths_row, token_positions):
    ends = jnp.cumsum(lengths_row)
    return jnp.sum((ends[None, :] <= token_positions[..., None]).astype(jnp.int32), axis=-1)


def moved(value, count, pairs):
    pairs = [(s, d) for s, d in pairs if 0 <= s < count and 0 <= d < count]
    if not pairs:
        return jnp.zeros_like(value)
    return lax.ppermute(value, "ctx", pairs)


def body(tokens, qkv_weight, doc_lengths, span_order):
    rows = tokens[0]
    token_count = rows.shape[0]
    query_key_value = jnp.dot(
        rows,
        lax.all_gather(qkv_weight, "seq", axis=1, tiled=True),
        preferred_element_type=jnp.float32,
    ).astype(jnp.bfloat16)
    lengths_row = doc_lengths[0]
    order_row = span_order[0]
    places_all = positions(order_row)
    my_index = lax.axis_index("ctx")
    devices = lax.axis_size("ctx")
    first_row = my_index * token_count
    token_positions = lax.dynamic_slice_in_dim(places_all, first_row, token_count)
    query_rows = apply_rotary(
        query_key_value[:, : QUERY_HEADS * HEAD_SIZE].astype(jnp.float32), token_positions
    ).astype(jnp.bfloat16)
    key_rows = apply_rotary(
        query_key_value[
            :, QUERY_HEADS * HEAD_SIZE : (QUERY_HEADS + KEY_VALUE_HEADS) * HEAD_SIZE
        ].astype(jnp.float32),
        token_positions,
    ).astype(jnp.bfloat16)
    value_rows = query_key_value[:, (QUERY_HEADS + KEY_VALUE_HEADS) * HEAD_SIZE :]
    key_cols = key_rows.shape[1]
    stacked = jnp.concatenate([key_rows, value_rows], axis=1)

    early_first = order_row[2 * my_index] < devices
    offset = jnp.where(early_first, 0, SPAN).astype(jnp.int32)
    early_rows = lax.dynamic_slice_in_dim(stacked, offset, SPAN, 0)
    late_rows = lax.dynamic_slice_in_dim(stacked, SPAN - offset, SPAN, 0)
    early_queries = lax.dynamic_slice_in_dim(query_rows, offset, SPAN, 0)
    late_queries = lax.dynamic_slice_in_dim(query_rows, SPAN - offset, SPAN, 0)

    count = devices
    early_blocks = [early_rows]
    late_blocks = [late_rows]
    for step in range(1, WINDOW + 1):
        early_blocks.append(moved(early_rows, count, [(d, d + step) for d in range(count)]))
        from_late = moved(late_rows, count, [(d, d - step) for d in range(count)])
        from_early = moved(
            early_rows, count, [(d, 2 * count - 1 - d - step) for d in range(count - step, count)]
        )
        late_blocks.append(jnp.where(my_index + step <= count - 1, from_late, from_early))
    early_keys = jnp.concatenate(early_blocks, axis=0)
    late_keys = jnp.concatenate(late_blocks, axis=0)
    key_blocks = jnp.stack([early_keys, late_keys])

    steps = jnp.arange(WINDOW + 1, dtype=jnp.int32)
    query_spans = jnp.stack([my_index, 2 * devices - 1 - my_index])
    key_spans = query_spans[:, None] - steps[None, :]
    ramp = jnp.arange(SPAN, dtype=jnp.int32)
    key_places = (key_spans[:, :, None] * SPAN + ramp).reshape(2, -1)
    key_ok = jnp.repeat(key_spans >= 0, SPAN, axis=1)
    query_places = query_spans[:, None] * SPAN + ramp[None, :]
    key_docs = documents(lengths_row, key_places)
    query_docs = documents(lengths_row, query_places)
    live = (
        (query_docs[:, :, None] == key_docs[:, None, :])
        & (key_places[:, None, :] <= query_places[:, :, None])
        & key_ok[:, None, :]
    )

    queries = jnp.stack([early_queries, late_queries]).reshape(
        2, SPAN, KEY_VALUE_HEADS, QUERY_PER_KV, HEAD_SIZE
    )
    keys = key_blocks[:, :, :key_cols].reshape(2, -1, KEY_VALUE_HEADS, HEAD_SIZE)
    values = key_blocks[:, :, key_cols:].reshape(2, -1, KEY_VALUE_HEADS, HEAD_SIZE)
    scores = (
        jnp.einsum("sqhgd,skhd->shgqk", queries, keys, preferred_element_type=jnp.float32)
        * 0.125
    )
    live = live[:, None, None]
    scores = jnp.where(live, scores, -1e30)
    top = jnp.max(scores, axis=-1, keepdims=True)
    weights = jnp.where(live, jnp.exp(scores - top), 0.0)
    total = jnp.sum(weights, axis=-1)
    summed = jnp.einsum(
        "shgqk,skhd->shgqd",
        weights.astype(jnp.bfloat16),
        values,
        preferred_element_type=jnp.float32,
    )
    outputs = summed / total[..., None]
    outputs = jnp.transpose(outputs, (0, 3, 1, 2, 4)).reshape(2, SPAN, QUERY_HEADS * HEAD_SIZE)
    outputs = outputs.astype(jnp.bfloat16)
    ordered = jnp.where(early_first, outputs, outputs[::-1]).reshape(
        token_count, QUERY_HEADS * HEAD_SIZE
    )
    return ordered[None]


def solution(mesh):
    placed = (P("seq", "ctx", None), P(None, "seq"), P("seq", None), P("seq", None))
    return jax.shard_map(
        body, mesh=mesh, in_specs=placed, out_specs=P("seq", "ctx", None), check_vma=False
    )
```

```python
import jax
import jax.numpy as jnp
from jax import lax
from jax.sharding import PartitionSpec as P

QUERY_HEADS = 16
KEY_VALUE_HEADS = 4
HEAD_SIZE = 64
QUERY_PER_KV = 4
SPAN = 64
DOC_MOST = 1024
WINDOW = DOC_MOST // SPAN


def apply_rotary(value_rows, token_positions):
    token_count = value_rows.shape[0]
    heads = value_rows.reshape(token_count, -1, HEAD_SIZE)
    half = HEAD_SIZE // 2
    freq = 500000.0 ** (-jnp.arange(half, dtype=jnp.float32) * 2.0 / HEAD_SIZE)
    angle = token_positions.astype(jnp.float32)[:, None] * freq[None, :]
    cosine = jnp.cos(angle)[:, None, :]
    sine = jnp.sin(angle)[:, None, :]
    first = heads[..., :half]
    second = heads[..., half:]
    turned = jnp.concatenate(
        [first * cosine - second * sine, second * cosine + first * sine], axis=-1
    )
    return turned.reshape(token_count, -1)


def positions(order_row):
    offsets = jnp.arange(SPAN, dtype=jnp.int32)
    return (order_row[:, None] * SPAN + offsets[None, :]).reshape(-1)


def documents(lengths_row, token_positions):
    ends = jnp.cumsum(lengths_row)
    return jnp.sum((ends[None, :] <= token_positions[..., None]).astype(jnp.int32), axis=-1)


def moved(value, count, pairs):
    pairs = [(s, d) for s, d in pairs if 0 <= s < count and 0 <= d < count]
    if not pairs:
        return jnp.zeros_like(value)
    return lax.ppermute(value, "ctx", pairs)


def body(tokens, qkv_weight, doc_lengths, span_order):
    rows = tokens[0]
    token_count = rows.shape[0]
    query_key_value = jnp.dot(
        rows,
        lax.all_gather(qkv_weight, "seq", axis=1, tiled=True),
        preferred_element_type=jnp.float32,
    ).astype(jnp.bfloat16)
    lengths_row = doc_lengths[0]
    order_row = span_order[0]
    places_all = positions(order_row)
    my_index = lax.axis_index("ctx")
    devices = lax.axis_size("ctx")
    first_row = my_index * token_count
    token_positions = lax.dynamic_slice_in_dim(places_all, first_row, token_count)
    query_rows = apply_rotary(
        query_key_value[:, : QUERY_HEADS * HEAD_SIZE].astype(jnp.float32), token_positions
    ).astype(jnp.bfloat16)
    key_rows = apply_rotary(
        query_key_value[
            :, QUERY_HEADS * HEAD_SIZE : (QUERY_HEADS + KEY_VALUE_HEADS) * HEAD_SIZE
        ].astype(jnp.float32),
        token_positions,
    ).astype(jnp.bfloat16)
    value_rows = query_key_value[:, (QUERY_HEADS + KEY_VALUE_HEADS) * HEAD_SIZE :]
    key_cols = key_rows.shape[1]
    stacked = jnp.concatenate([key_rows, value_rows], axis=1)

    early_first = order_row[2 * my_index] < devices
    offset = jnp.where(early_first, 0, SPAN).astype(jnp.int32)
    early_rows = lax.dynamic_slice_in_dim(stacked, offset, SPAN, 0)
    late_rows = lax.dynamic_slice_in_dim(stacked, SPAN - offset, SPAN, 0)
    early_queries = lax.dynamic_slice_in_dim(query_rows, offset, SPAN, 0)
    late_queries = lax.dynamic_slice_in_dim(query_rows, SPAN - offset, SPAN, 0)

    count = devices
    up = early_rows[None]
    down = jnp.stack([early_rows, late_rows])[None]
    reach = 1
    while reach < WINDOW:
        up = jnp.concatenate(
            [up, moved(up, count, [(d, d + reach) for d in range(count)])], axis=0
        )
        down = jnp.concatenate(
            [down, moved(down, count, [(d, d - reach) for d in range(count)])], axis=0
        )
        reach *= 2
    up = jnp.concatenate(
        [up, moved(early_rows[None], count, [(d, d + WINDOW) for d in range(count)])], axis=0
    )
    down = jnp.concatenate(
        [down, moved(down[:1], count, [(d, d - WINDOW) for d in range(count)])], axis=0
    )
    early_keys = up.reshape(-1, up.shape[-1])
    around = jnp.concatenate([up[::-1], down[1:, 0]], axis=0)
    steps = jnp.arange(WINDOW + 1, dtype=jnp.int32)
    mirror = jnp.clip(2 * count - 1 - 2 * my_index - steps + WINDOW, 0, 2 * WINDOW)
    late_keys = jnp.where(
        (my_index + steps <= count - 1)[:, None, None], down[:, 1], jnp.take(around, mirror, axis=0)
    ).reshape(-1, up.shape[-1])
    key_blocks = jnp.stack([early_keys, late_keys])

    steps = jnp.arange(WINDOW + 1, dtype=jnp.int32)
    query_spans = jnp.stack([my_index, 2 * devices - 1 - my_index])
    key_spans = query_spans[:, None] - steps[None, :]
    ramp = jnp.arange(SPAN, dtype=jnp.int32)
    key_places = (key_spans[:, :, None] * SPAN + ramp).reshape(2, -1)
    key_ok = jnp.repeat(key_spans >= 0, SPAN, axis=1)
    query_places = query_spans[:, None] * SPAN + ramp[None, :]
    key_docs = documents(lengths_row, key_places)
    query_docs = documents(lengths_row, query_places)
    live = (
        (query_docs[:, :, None] == key_docs[:, None, :])
        & (key_places[:, None, :] <= query_places[:, :, None])
        & key_ok[:, None, :]
    )

    queries = jnp.stack([early_queries, late_queries]).reshape(
        2, SPAN, KEY_VALUE_HEADS, QUERY_PER_KV, HEAD_SIZE
    )
    keys = key_blocks[:, :, :key_cols].reshape(2, -1, KEY_VALUE_HEADS, HEAD_SIZE)
    values = key_blocks[:, :, key_cols:].reshape(2, -1, KEY_VALUE_HEADS, HEAD_SIZE)
    scores = (
        jnp.einsum("sqhgd,skhd->shgqk", queries, keys, preferred_element_type=jnp.float32)
        * 0.125
    )
    live = live[:, None, None]
    scores = jnp.where(live, scores, -1e30)
    top = jnp.max(scores, axis=-1, keepdims=True)
    weights = jnp.where(live, jnp.exp(scores - top), 0.0)
    total = jnp.sum(weights, axis=-1)
    summed = jnp.einsum(
        "shgqk,skhd->shgqd",
        weights.astype(jnp.bfloat16),
        values,
        preferred_element_type=jnp.float32,
    )
    outputs = summed / total[..., None]
    outputs = jnp.transpose(outputs, (0, 3, 1, 2, 4)).reshape(2, SPAN, QUERY_HEADS * HEAD_SIZE)
    outputs = outputs.astype(jnp.bfloat16)
    ordered = jnp.where(early_first, outputs, outputs[::-1]).reshape(
        token_count, QUERY_HEADS * HEAD_SIZE
    )
    return ordered[None]


def solution(mesh):
    placed = (P("seq", "ctx", None), P(None, "seq"), P("seq", None), P("seq", None))
    return jax.shard_map(
        body, mesh=mesh, in_specs=placed, out_specs=P("seq", "ctx", None), check_vma=False
    )
```

```python
import jax
import jax.numpy as jnp
from jax import lax
from jax.sharding import PartitionSpec as P

QUERY_HEADS = 16
KEY_VALUE_HEADS = 4
HEAD_SIZE = 64
QUERY_PER_KV = 4
SPAN = 64
DOC_MOST = 1024
WINDOW = DOC_MOST // SPAN


def apply_rotary(value_rows, token_positions):
    token_count = value_rows.shape[0]
    heads = value_rows.reshape(token_count, -1, HEAD_SIZE)
    half = HEAD_SIZE // 2
    freq = 500000.0 ** (-jnp.arange(half, dtype=jnp.float32) * 2.0 / HEAD_SIZE)
    angle = token_positions.astype(jnp.float32)[:, None] * freq[None, :]
    cosine = jnp.cos(angle)[:, None, :]
    sine = jnp.sin(angle)[:, None, :]
    first = heads[..., :half]
    second = heads[..., half:]
    turned = jnp.concatenate(
        [first * cosine - second * sine, second * cosine + first * sine], axis=-1
    )
    return turned.reshape(token_count, -1)


def positions(order_row):
    offsets = jnp.arange(SPAN, dtype=jnp.int32)
    return (order_row[:, None] * SPAN + offsets[None, :]).reshape(-1)


def documents(lengths_row, token_positions):
    ends = jnp.cumsum(lengths_row)
    return jnp.sum((ends[None, :] <= token_positions[..., None]).astype(jnp.int32), axis=-1)


def moved(value, count, pairs):
    pairs = [(s, d) for s, d in pairs if 0 <= s < count and 0 <= d < count]
    if not pairs:
        return jnp.zeros_like(value)
    return lax.ppermute(value, "ctx", pairs)


def body(tokens, qkv_weight, doc_lengths, span_order):
    rows = tokens[0]
    token_count = rows.shape[0]
    query_key_value = jnp.dot(
        rows,
        lax.all_gather(qkv_weight, "seq", axis=1, tiled=True),
        preferred_element_type=jnp.float32,
    ).astype(jnp.bfloat16)
    lengths_row = doc_lengths[0]
    order_row = span_order[0]
    places_all = positions(order_row)
    my_index = lax.axis_index("ctx")
    devices = lax.axis_size("ctx")
    first_row = my_index * token_count
    token_positions = lax.dynamic_slice_in_dim(places_all, first_row, token_count)
    query_rows = apply_rotary(
        query_key_value[:, : QUERY_HEADS * HEAD_SIZE].astype(jnp.float32), token_positions
    ).astype(jnp.bfloat16)
    key_rows = apply_rotary(
        query_key_value[
            :, QUERY_HEADS * HEAD_SIZE : (QUERY_HEADS + KEY_VALUE_HEADS) * HEAD_SIZE
        ].astype(jnp.float32),
        token_positions,
    ).astype(jnp.bfloat16)
    value_rows = query_key_value[:, (QUERY_HEADS + KEY_VALUE_HEADS) * HEAD_SIZE :]
    key_cols = key_rows.shape[1]
    stacked = jnp.concatenate([key_rows, value_rows], axis=1)

    early_first = order_row[2 * my_index] < devices
    offset = jnp.where(early_first, 0, SPAN).astype(jnp.int32)
    early_rows = lax.dynamic_slice_in_dim(stacked, offset, SPAN, 0)
    late_rows = lax.dynamic_slice_in_dim(stacked, SPAN - offset, SPAN, 0)
    early_queries = lax.dynamic_slice_in_dim(query_rows, offset, SPAN, 0)
    late_queries = lax.dynamic_slice_in_dim(query_rows, SPAN - offset, SPAN, 0)

    count = devices
    region = range(count - WINDOW // 2, count)
    up = early_rows[None]
    down = late_rows[None]
    mirror = early_rows[None]
    reach = 1
    while reach < WINDOW:
        up = jnp.concatenate(
            [up, moved(up, count, [(d, d + reach) for d in range(count)])], axis=0
        )
        down = jnp.concatenate(
            [down, moved(down, count, [(d, d - reach) for d in range(count)])], axis=0
        )
        if reach < WINDOW // 2:
            mirror = jnp.concatenate(
                [mirror, moved(mirror, count, [(d, d - reach) for d in region if d - reach in region])],
                axis=0,
            )
        reach *= 2
    up = jnp.concatenate(
        [up, moved(early_rows[None], count, [(d, d + WINDOW) for d in range(count)])], axis=0
    )
    down = jnp.concatenate(
        [down, moved(late_rows[None], count, [(d, d - WINDOW) for d in range(count)])], axis=0
    )
    crossed = moved(mirror, count, [(d, 2 * count - 1 - WINDOW - d) for d in region])
    inside = my_index >= count - WINDOW // 2
    mirror = jnp.where(inside, mirror, crossed)
    base = jnp.where(inside, my_index, 2 * count - 1 - WINDOW - my_index)
    around = jnp.concatenate([up, mirror, down], axis=0)
    steps = jnp.arange(WINDOW + 1, dtype=jnp.int32)
    target = 2 * count - 1 - my_index - steps
    pick = jnp.where(
        my_index + steps <= count - 1,
        up.shape[0] + mirror.shape[0] + steps,
        jnp.where(target >= base, up.shape[0] + target - base, my_index - target),
    )
    pick = jnp.clip(pick, 0, around.shape[0] - 1)
    early_keys = up.reshape(-1, up.shape[-1])
    late_keys = jnp.take(around, pick, axis=0).reshape(-1, up.shape[-1])
    key_blocks = jnp.stack([early_keys, late_keys])

    steps = jnp.arange(WINDOW + 1, dtype=jnp.int32)
    query_spans = jnp.stack([my_index, 2 * devices - 1 - my_index])
    key_spans = query_spans[:, None] - steps[None, :]
    ramp = jnp.arange(SPAN, dtype=jnp.int32)
    key_places = (key_spans[:, :, None] * SPAN + ramp).reshape(2, -1)
    key_ok = jnp.repeat(key_spans >= 0, SPAN, axis=1)
    query_places = query_spans[:, None] * SPAN + ramp[None, :]
    key_docs = documents(lengths_row, key_places)
    query_docs = documents(lengths_row, query_places)
    live = (
        (query_docs[:, :, None] == key_docs[:, None, :])
        & (key_places[:, None, :] <= query_places[:, :, None])
        & key_ok[:, None, :]
    )

    queries = jnp.stack([early_queries, late_queries]).reshape(
        2, SPAN, KEY_VALUE_HEADS, QUERY_PER_KV, HEAD_SIZE
    )
    keys = key_blocks[:, :, :key_cols].reshape(2, -1, KEY_VALUE_HEADS, HEAD_SIZE)
    values = key_blocks[:, :, key_cols:].reshape(2, -1, KEY_VALUE_HEADS, HEAD_SIZE)
    scores = (
        jnp.einsum("sqhgd,skhd->shgqk", queries, keys, preferred_element_type=jnp.float32)
        * 0.125
    )
    live = live[:, None, None]
    scores = jnp.where(live, scores, -1e30)
    top = jnp.max(scores, axis=-1, keepdims=True)
    weights = jnp.where(live, jnp.exp(scores - top), 0.0)
    total = jnp.sum(weights, axis=-1)
    summed = jnp.einsum(
        "shgqk,skhd->shgqd",
        weights.astype(jnp.bfloat16),
        values,
        preferred_element_type=jnp.float32,
    )
    outputs = summed / total[..., None]
    outputs = jnp.transpose(outputs, (0, 3, 1, 2, 4)).reshape(2, SPAN, QUERY_HEADS * HEAD_SIZE)
    outputs = outputs.astype(jnp.bfloat16)
    ordered = jnp.where(early_first, outputs, outputs[::-1]).reshape(
        token_count, QUERY_HEADS * HEAD_SIZE
    )
    return ordered[None]


def solution(mesh):
    placed = (P("seq", "ctx", None), P(None, "seq"), P("seq", None), P("seq", None))
    return jax.shard_map(
        body, mesh=mesh, in_specs=placed, out_specs=P("seq", "ctx", None), check_vma=False
    )
```

```python
import jax
import jax.numpy as jnp
from jax import lax
from jax.sharding import PartitionSpec as P

QUERY_HEADS = 16
KEY_VALUE_HEADS = 4
HEAD_SIZE = 64
QUERY_PER_KV = 4
SPAN = 64
DOC_MOST = 1024
WINDOW = DOC_MOST // SPAN


def apply_rotary(value_rows, token_positions):
    token_count = value_rows.shape[0]
    heads = value_rows.reshape(token_count, -1, HEAD_SIZE)
    half = HEAD_SIZE // 2
    freq = 500000.0 ** (-jnp.arange(half, dtype=jnp.float32) * 2.0 / HEAD_SIZE)
    angle = token_positions.astype(jnp.float32)[:, None] * freq[None, :]
    cosine = jnp.cos(angle)[:, None, :]
    sine = jnp.sin(angle)[:, None, :]
    first = heads[..., :half]
    second = heads[..., half:]
    turned = jnp.concatenate(
        [first * cosine - second * sine, second * cosine + first * sine], axis=-1
    )
    return turned.reshape(token_count, -1)


def positions(order_row):
    offsets = jnp.arange(SPAN, dtype=jnp.int32)
    return (order_row[:, None] * SPAN + offsets[None, :]).reshape(-1)


def documents(lengths_row, token_positions):
    ends = jnp.cumsum(lengths_row)
    return jnp.sum((ends[None, :] <= token_positions[..., None]).astype(jnp.int32), axis=-1)


def moved(value, count, pairs):
    pairs = [(s, d) for s, d in pairs if 0 <= s < count and 0 <= d < count]
    if not pairs:
        return jnp.zeros_like(value)
    return lax.ppermute(value, "ctx", pairs)


def body(tokens, qkv_weight, doc_lengths, span_order):
    rows = tokens[0]
    token_count = rows.shape[0]
    query_key_value = jnp.dot(
        rows,
        lax.all_gather(qkv_weight, "seq", axis=1, tiled=True),
        preferred_element_type=jnp.float32,
    ).astype(jnp.bfloat16)
    lengths_row = doc_lengths[0]
    order_row = span_order[0]
    places_all = positions(order_row)
    my_index = lax.axis_index("ctx")
    devices = lax.axis_size("ctx")
    first_row = my_index * token_count
    token_positions = lax.dynamic_slice_in_dim(places_all, first_row, token_count)
    query_rows = apply_rotary(
        query_key_value[:, : QUERY_HEADS * HEAD_SIZE].astype(jnp.float32), token_positions
    ).astype(jnp.bfloat16)
    key_rows = apply_rotary(
        query_key_value[
            :, QUERY_HEADS * HEAD_SIZE : (QUERY_HEADS + KEY_VALUE_HEADS) * HEAD_SIZE
        ].astype(jnp.float32),
        token_positions,
    ).astype(jnp.bfloat16)
    value_rows = query_key_value[:, (QUERY_HEADS + KEY_VALUE_HEADS) * HEAD_SIZE :]
    key_cols = key_rows.shape[1]
    stacked = jnp.concatenate([key_rows, value_rows], axis=1)

    early_first = order_row[2 * my_index] < devices
    offset = jnp.where(early_first, 0, SPAN).astype(jnp.int32)
    early_rows = lax.dynamic_slice_in_dim(stacked, offset, SPAN, 0)
    late_rows = lax.dynamic_slice_in_dim(stacked, SPAN - offset, SPAN, 0)
    early_queries = lax.dynamic_slice_in_dim(query_rows, offset, SPAN, 0)
    late_queries = lax.dynamic_slice_in_dim(query_rows, SPAN - offset, SPAN, 0)

    count = devices
    up = early_rows[None]
    down = jnp.stack([early_rows, late_rows])[None]
    reach = 1
    while reach < WINDOW:
        up = jnp.concatenate(
            [up, moved(up, count, [(d, d + reach) for d in range(count)])], axis=0
        )
        if 2 * reach < WINDOW:
            got = moved(down, count, [(d, d - reach) for d in range(count)])
        else:
            tail = range(count - reach, count)
            got = jnp.stack(
                [
                    moved(down[:, 0], count, [(d, d - reach) for d in tail]),
                    moved(down[:, 1], count, [(d, d - reach) for d in range(count)]),
                ],
                axis=1,
            )
        down = jnp.concatenate([down, got], axis=0)
        reach *= 2
    up = jnp.concatenate(
        [up, moved(early_rows[None], count, [(d, d + WINDOW) for d in range(count)])], axis=0
    )
    far = moved(late_rows[None], count, [(d, d - WINDOW) for d in range(count)])
    down = jnp.concatenate([down, jnp.stack([jnp.zeros_like(far), far], axis=1)], axis=0)
    early_keys = up.reshape(-1, up.shape[-1])
    around = jnp.concatenate([up[::-1], down[1:, 0]], axis=0)
    steps = jnp.arange(WINDOW + 1, dtype=jnp.int32)
    mirror = jnp.clip(2 * count - 1 - 2 * my_index - steps + WINDOW, 0, 2 * WINDOW)
    late_keys = jnp.where(
        (my_index + steps <= count - 1)[:, None, None], down[:, 1], jnp.take(around, mirror, axis=0)
    ).reshape(-1, up.shape[-1])
    key_blocks = jnp.stack([early_keys, late_keys])

    steps = jnp.arange(WINDOW + 1, dtype=jnp.int32)
    query_spans = jnp.stack([my_index, 2 * devices - 1 - my_index])
    key_spans = query_spans[:, None] - steps[None, :]
    ramp = jnp.arange(SPAN, dtype=jnp.int32)
    key_places = (key_spans[:, :, None] * SPAN + ramp).reshape(2, -1)
    key_ok = jnp.repeat(key_spans >= 0, SPAN, axis=1)
    query_places = query_spans[:, None] * SPAN + ramp[None, :]
    key_docs = documents(lengths_row, key_places)
    query_docs = documents(lengths_row, query_places)
    live = (
        (query_docs[:, :, None] == key_docs[:, None, :])
        & (key_places[:, None, :] <= query_places[:, :, None])
        & key_ok[:, None, :]
    )

    queries = jnp.stack([early_queries, late_queries]).reshape(
        2, SPAN, KEY_VALUE_HEADS, QUERY_PER_KV, HEAD_SIZE
    )
    keys = key_blocks[:, :, :key_cols].reshape(2, -1, KEY_VALUE_HEADS, HEAD_SIZE)
    values = key_blocks[:, :, key_cols:].reshape(2, -1, KEY_VALUE_HEADS, HEAD_SIZE)
    scores = (
        jnp.einsum("sqhgd,skhd->shgqk", queries, keys, preferred_element_type=jnp.float32)
        * 0.125
    )
    live = live[:, None, None]
    scores = jnp.where(live, scores, -1e30)
    top = jnp.max(scores, axis=-1, keepdims=True)
    weights = jnp.where(live, jnp.exp(scores - top), 0.0)
    total = jnp.sum(weights, axis=-1)
    summed = jnp.einsum(
        "shgqk,skhd->shgqd",
        weights.astype(jnp.bfloat16),
        values,
        preferred_element_type=jnp.float32,
    )
    outputs = summed / total[..., None]
    outputs = jnp.transpose(outputs, (0, 3, 1, 2, 4)).reshape(2, SPAN, QUERY_HEADS * HEAD_SIZE)
    outputs = outputs.astype(jnp.bfloat16)
    ordered = jnp.where(early_first, outputs, outputs[::-1]).reshape(
        token_count, QUERY_HEADS * HEAD_SIZE
    )
    return ordered[None]


def solution(mesh):
    placed = (P("seq", "ctx", None), P(None, "seq"), P("seq", None), P("seq", None))
    return jax.shard_map(
        body, mesh=mesh, in_specs=placed, out_specs=P("seq", "ctx", None), check_vma=False
    )
```

```python
import jax
import jax.numpy as jnp
from jax import lax
from jax.sharding import PartitionSpec as P

QUERY_HEADS = 16
KEY_VALUE_HEADS = 4
HEAD_SIZE = 64
QUERY_PER_KV = 4
SPAN = 64
DOC_MOST = 1024
WINDOW = DOC_MOST // SPAN


def apply_rotary(value_rows, token_positions):
    token_count = value_rows.shape[0]
    heads = value_rows.reshape(token_count, -1, HEAD_SIZE)
    half = HEAD_SIZE // 2
    freq = 500000.0 ** (-jnp.arange(half, dtype=jnp.float32) * 2.0 / HEAD_SIZE)
    angle = token_positions.astype(jnp.float32)[:, None] * freq[None, :]
    cosine = jnp.cos(angle)[:, None, :]
    sine = jnp.sin(angle)[:, None, :]
    first = heads[..., :half]
    second = heads[..., half:]
    turned = jnp.concatenate(
        [first * cosine - second * sine, second * cosine + first * sine], axis=-1
    )
    return turned.reshape(token_count, -1)


def positions(order_row):
    offsets = jnp.arange(SPAN, dtype=jnp.int32)
    return (order_row[:, None] * SPAN + offsets[None, :]).reshape(-1)


def documents(lengths_row, token_positions):
    ends = jnp.cumsum(lengths_row)
    return jnp.sum((ends[None, :] <= token_positions[..., None]).astype(jnp.int32), axis=-1)


def moved(value, count, pairs):
    pairs = [(s, d) for s, d in pairs if 0 <= s < count and 0 <= d < count]
    if not pairs:
        return jnp.zeros_like(value)
    return lax.ppermute(value, "ctx", pairs)


def chip_of(index, lanes):
    line, core = divmod(index // lanes, 2)
    half, rest = divmod(index % lanes, lanes // 2)
    return line, core, half, rest


def device_of(line, core, half, rest, lanes, lines):
    return (2 * line + core) * lanes + half * (lanes // 2) + rest


def project(rows, weight):
    lines = lax.axis_size("seq") // 2
    lanes = lax.axis_size("ctx")
    total = 2 * lines * lanes
    both = ("seq", "ctx")

    def pairs_for(offset):
        found = []
        for dest in range(total):
            line, core, half, rest = chip_of(dest, lanes)
            level = half * lines + line + offset(core)
            level %= 2 * lines
            found.append((device_of(level % lines, core, level // lines, rest, lanes, lines), dest))
        return found

    def mate_pairs():
        found = []
        for dest in range(total):
            line, core, half, rest = chip_of(dest, lanes)
            found.append((device_of(line, 1 - core, half, rest, lanes, lines), dest))
        return found

    step = [lambda core: 0]
    for shift in range(1, lines):
        if 2 * shift == lines:
            step.append(lambda core, s=shift: s if core == 0 else -s)
        elif 2 * shift < lines:
            step.append(lambda core, s=shift: s)
        else:
            step.append(lambda core, s=shift: s - lines)
    mine = [weight] + [lax.ppermute(weight, both, pairs_for(f)) for f in step[1:]]
    mine = jnp.stack(mine)
    mate = lax.ppermute(mine, both, mate_pairs())
    blocks = jnp.concatenate([mine, mate], axis=0)
    seq_index = lax.axis_index("seq")
    line, core = seq_index // 2, seq_index % 2
    wanted = jnp.arange(2 * lines, dtype=jnp.int32)
    slot = (wanted // 2 - line) % lines + lines * (wanted % 2 != core).astype(jnp.int32)
    ordered = jnp.take(blocks, slot, axis=0)
    full = jnp.transpose(ordered, (1, 0, 2)).reshape(weight.shape[0], -1)
    return jnp.dot(rows, full, preferred_element_type=jnp.float32).astype(jnp.bfloat16)


def body(tokens, qkv_weight, doc_lengths, span_order):
    rows = tokens[0]
    token_count = rows.shape[0]
    query_key_value = project(rows, qkv_weight)
    lengths_row = doc_lengths[0]
    order_row = span_order[0]
    places_all = positions(order_row)
    my_index = lax.axis_index("ctx")
    devices = lax.axis_size("ctx")
    first_row = my_index * token_count
    token_positions = lax.dynamic_slice_in_dim(places_all, first_row, token_count)
    query_rows = apply_rotary(
        query_key_value[:, : QUERY_HEADS * HEAD_SIZE].astype(jnp.float32), token_positions
    ).astype(jnp.bfloat16)
    key_rows = apply_rotary(
        query_key_value[
            :, QUERY_HEADS * HEAD_SIZE : (QUERY_HEADS + KEY_VALUE_HEADS) * HEAD_SIZE
        ].astype(jnp.float32),
        token_positions,
    ).astype(jnp.bfloat16)
    value_rows = query_key_value[:, (QUERY_HEADS + KEY_VALUE_HEADS) * HEAD_SIZE :]
    key_cols = key_rows.shape[1]
    stacked = jnp.concatenate([key_rows, value_rows], axis=1)

    early_first = order_row[2 * my_index] < devices
    offset = jnp.where(early_first, 0, SPAN).astype(jnp.int32)
    early_rows = lax.dynamic_slice_in_dim(stacked, offset, SPAN, 0)
    late_rows = lax.dynamic_slice_in_dim(stacked, SPAN - offset, SPAN, 0)
    early_queries = lax.dynamic_slice_in_dim(query_rows, offset, SPAN, 0)
    late_queries = lax.dynamic_slice_in_dim(query_rows, SPAN - offset, SPAN, 0)

    count = devices
    up = early_rows[None]
    down = jnp.stack([early_rows, late_rows])[None]
    reach = 1
    while reach < WINDOW:
        up = jnp.concatenate(
            [up, moved(up, count, [(d, d + reach) for d in range(count)])], axis=0
        )
        if 2 * reach < WINDOW:
            got = moved(down, count, [(d, d - reach) for d in range(count)])
        else:
            tail = range(count - reach, count)
            got = jnp.stack(
                [
                    moved(down[:, 0], count, [(d, d - reach) for d in tail]),
                    moved(down[:, 1], count, [(d, d - reach) for d in range(count)]),
                ],
                axis=1,
            )
        down = jnp.concatenate([down, got], axis=0)
        reach *= 2
    up = jnp.concatenate(
        [up, moved(early_rows[None], count, [(d, d + WINDOW) for d in range(count)])], axis=0
    )
    far = moved(late_rows[None], count, [(d, d - WINDOW) for d in range(count)])
    down = jnp.concatenate([down, jnp.stack([jnp.zeros_like(far), far], axis=1)], axis=0)
    early_keys = up.reshape(-1, up.shape[-1])
    around = jnp.concatenate([up[::-1], down[1:, 0]], axis=0)
    steps = jnp.arange(WINDOW + 1, dtype=jnp.int32)
    mirror = jnp.clip(2 * count - 1 - 2 * my_index - steps + WINDOW, 0, 2 * WINDOW)
    late_keys = jnp.where(
        (my_index + steps <= count - 1)[:, None, None], down[:, 1], jnp.take(around, mirror, axis=0)
    ).reshape(-1, up.shape[-1])
    key_blocks = jnp.stack([early_keys, late_keys])

    steps = jnp.arange(WINDOW + 1, dtype=jnp.int32)
    query_spans = jnp.stack([my_index, 2 * devices - 1 - my_index])
    key_spans = query_spans[:, None] - steps[None, :]
    ramp = jnp.arange(SPAN, dtype=jnp.int32)
    key_places = (key_spans[:, :, None] * SPAN + ramp).reshape(2, -1)
    key_ok = jnp.repeat(key_spans >= 0, SPAN, axis=1)
    query_places = query_spans[:, None] * SPAN + ramp[None, :]
    key_docs = documents(lengths_row, key_places)
    query_docs = documents(lengths_row, query_places)
    live = (
        (query_docs[:, :, None] == key_docs[:, None, :])
        & (key_places[:, None, :] <= query_places[:, :, None])
        & key_ok[:, None, :]
    )

    queries = jnp.stack([early_queries, late_queries]).reshape(
        2, SPAN, KEY_VALUE_HEADS, QUERY_PER_KV, HEAD_SIZE
    )
    keys = key_blocks[:, :, :key_cols].reshape(2, -1, KEY_VALUE_HEADS, HEAD_SIZE)
    values = key_blocks[:, :, key_cols:].reshape(2, -1, KEY_VALUE_HEADS, HEAD_SIZE)
    scores = (
        jnp.einsum("sqhgd,skhd->shgqk", queries, keys, preferred_element_type=jnp.float32)
        * 0.125
    )
    live = live[:, None, None]
    scores = jnp.where(live, scores, -1e30)
    top = jnp.max(scores, axis=-1, keepdims=True)
    weights = jnp.where(live, jnp.exp(scores - top), 0.0)
    total = jnp.sum(weights, axis=-1)
    summed = jnp.einsum(
        "shgqk,skhd->shgqd",
        weights.astype(jnp.bfloat16),
        values,
        preferred_element_type=jnp.float32,
    )
    outputs = summed / total[..., None]
    outputs = jnp.transpose(outputs, (0, 3, 1, 2, 4)).reshape(2, SPAN, QUERY_HEADS * HEAD_SIZE)
    outputs = outputs.astype(jnp.bfloat16)
    ordered = jnp.where(early_first, outputs, outputs[::-1]).reshape(
        token_count, QUERY_HEADS * HEAD_SIZE
    )
    return ordered[None]


def solution(mesh):
    placed = (P("seq", "ctx", None), P(None, "seq"), P("seq", None), P("seq", None))
    return jax.shard_map(
        body, mesh=mesh, in_specs=placed, out_specs=P("seq", "ctx", None), check_vma=False
    )
```

```python
import jax
import jax.numpy as jnp
from jax import lax
from jax.sharding import PartitionSpec as P

QUERY_HEADS = 16
KEY_VALUE_HEADS = 4
HEAD_SIZE = 64
QUERY_PER_KV = 4
SPAN = 64
DOC_MOST = 1024
WINDOW = DOC_MOST // SPAN


def apply_rotary(value_rows, token_positions):
    token_count = value_rows.shape[0]
    heads = value_rows.reshape(token_count, -1, HEAD_SIZE)
    half = HEAD_SIZE // 2
    freq = 500000.0 ** (-jnp.arange(half, dtype=jnp.float32) * 2.0 / HEAD_SIZE)
    angle = token_positions.astype(jnp.float32)[:, None] * freq[None, :]
    cosine = jnp.cos(angle)[:, None, :]
    sine = jnp.sin(angle)[:, None, :]
    first = heads[..., :half]
    second = heads[..., half:]
    turned = jnp.concatenate(
        [first * cosine - second * sine, second * cosine + first * sine], axis=-1
    )
    return turned.reshape(token_count, -1)


def positions(order_row):
    offsets = jnp.arange(SPAN, dtype=jnp.int32)
    return (order_row[:, None] * SPAN + offsets[None, :]).reshape(-1)


def documents(lengths_row, token_positions):
    ends = jnp.cumsum(lengths_row)
    return jnp.sum((ends[None, :] <= token_positions[..., None]).astype(jnp.int32), axis=-1)


def moved(value, count, pairs):
    pairs = [(s, d) for s, d in pairs if 0 <= s < count and 0 <= d < count]
    if not pairs:
        return jnp.zeros_like(value)
    return lax.ppermute(value, "ctx", pairs)


def chip_of(index, lanes):
    line, core = divmod(index // lanes, 2)
    half, rest = divmod(index % lanes, lanes // 2)
    return line, core, half, rest


def device_of(line, core, half, rest, lanes, lines):
    return (2 * line + core) * lanes + half * (lanes // 2) + rest


def project(rows, weight):
    lines = lax.axis_size("seq") // 2
    lanes = lax.axis_size("ctx")
    total = 2 * lines * lanes
    both = ("seq", "ctx")

    def pairs_for(offset):
        found = []
        for dest in range(total):
            line, core, half, rest = chip_of(dest, lanes)
            level = half * lines + line + offset(core)
            level %= 2 * lines
            found.append((device_of(level % lines, core, level // lines, rest, lanes, lines), dest))
        return found

    def mate_pairs():
        found = []
        for dest in range(total):
            line, core, half, rest = chip_of(dest, lanes)
            found.append((device_of(line, 1 - core, half, rest, lanes, lines), dest))
        return found

    step = [lambda core: 0]
    for shift in range(1, lines):
        if 2 * shift == lines:
            step.append(lambda core, s=shift: s if core == 0 else -s)
        elif 2 * shift < lines:
            step.append(lambda core, s=shift: s)
        else:
            step.append(lambda core, s=shift: s - lines)
    mine = [weight] + [lax.ppermute(weight, both, pairs_for(f)) for f in step[1:]]
    mate = lax.ppermute(jnp.stack(mine), both, mate_pairs())
    parts = [jnp.dot(rows, block, preferred_element_type=jnp.float32) for block in mine]
    parts += [
        jnp.dot(rows, mate[index], preferred_element_type=jnp.float32) for index in range(len(mine))
    ]
    parts = jnp.stack(parts).astype(jnp.bfloat16)
    seq_index = lax.axis_index("seq")
    line, core = seq_index // 2, seq_index % 2
    wanted = jnp.arange(2 * lines, dtype=jnp.int32)
    slot = (wanted // 2 - line) % lines + lines * (wanted % 2 != core).astype(jnp.int32)
    ordered = jnp.take(parts, slot, axis=0)
    return jnp.transpose(ordered, (1, 0, 2)).reshape(rows.shape[0], -1)


def body(tokens, qkv_weight, doc_lengths, span_order):
    rows = tokens[0]
    token_count = rows.shape[0]
    query_key_value = project(rows, qkv_weight)
    lengths_row = doc_lengths[0]
    order_row = span_order[0]
    places_all = positions(order_row)
    my_index = lax.axis_index("ctx")
    devices = lax.axis_size("ctx")
    first_row = my_index * token_count
    token_positions = lax.dynamic_slice_in_dim(places_all, first_row, token_count)
    query_rows = apply_rotary(
        query_key_value[:, : QUERY_HEADS * HEAD_SIZE].astype(jnp.float32), token_positions
    ).astype(jnp.bfloat16)
    key_rows = apply_rotary(
        query_key_value[
            :, QUERY_HEADS * HEAD_SIZE : (QUERY_HEADS + KEY_VALUE_HEADS) * HEAD_SIZE
        ].astype(jnp.float32),
        token_positions,
    ).astype(jnp.bfloat16)
    value_rows = query_key_value[:, (QUERY_HEADS + KEY_VALUE_HEADS) * HEAD_SIZE :]
    key_cols = key_rows.shape[1]
    stacked = jnp.concatenate([key_rows, value_rows], axis=1)

    early_first = order_row[2 * my_index] < devices
    offset = jnp.where(early_first, 0, SPAN).astype(jnp.int32)
    early_rows = lax.dynamic_slice_in_dim(stacked, offset, SPAN, 0)
    late_rows = lax.dynamic_slice_in_dim(stacked, SPAN - offset, SPAN, 0)
    early_queries = lax.dynamic_slice_in_dim(query_rows, offset, SPAN, 0)
    late_queries = lax.dynamic_slice_in_dim(query_rows, SPAN - offset, SPAN, 0)

    count = devices
    up = early_rows[None]
    down = jnp.stack([early_rows, late_rows])[None]
    reach = 1
    while reach < WINDOW:
        up = jnp.concatenate(
            [up, moved(up, count, [(d, d + reach) for d in range(count)])], axis=0
        )
        if 2 * reach < WINDOW:
            got = moved(down, count, [(d, d - reach) for d in range(count)])
        else:
            tail = range(count - reach, count)
            got = jnp.stack(
                [
                    moved(down[:, 0], count, [(d, d - reach) for d in tail]),
                    moved(down[:, 1], count, [(d, d - reach) for d in range(count)]),
                ],
                axis=1,
            )
        down = jnp.concatenate([down, got], axis=0)
        reach *= 2
    up = jnp.concatenate(
        [up, moved(early_rows[None], count, [(d, d + WINDOW) for d in range(count)])], axis=0
    )
    far = moved(late_rows[None], count, [(d, d - WINDOW) for d in range(count)])
    down = jnp.concatenate([down, jnp.stack([jnp.zeros_like(far), far], axis=1)], axis=0)
    early_keys = up.reshape(-1, up.shape[-1])
    around = jnp.concatenate([up, down[:, 0], down[:, 1]], axis=0)
    steps = jnp.arange(WINDOW + 1, dtype=jnp.int32)
    source = 2 * count - 1 - my_index - steps
    pick = jnp.where(
        my_index + steps <= count - 1,
        2 * (WINDOW + 1) + steps,
        jnp.where(source <= my_index, my_index - source, WINDOW + 1 + source - my_index),
    )
    pick = jnp.clip(pick, 0, around.shape[0] - 1)
    late_keys = jnp.take(around, pick, axis=0).reshape(-1, up.shape[-1])
    key_blocks = jnp.stack([early_keys, late_keys])

    steps = jnp.arange(WINDOW + 1, dtype=jnp.int32)
    query_spans = jnp.stack([my_index, 2 * devices - 1 - my_index])
    key_spans = query_spans[:, None] - steps[None, :]
    ramp = jnp.arange(SPAN, dtype=jnp.int32)
    key_places = (key_spans[:, :, None] * SPAN + ramp).reshape(2, -1)
    key_ok = jnp.repeat(key_spans >= 0, SPAN, axis=1)
    query_places = query_spans[:, None] * SPAN + ramp[None, :]
    key_docs = documents(lengths_row, key_places)
    query_docs = documents(lengths_row, query_places)
    live = (
        (query_docs[:, :, None] == key_docs[:, None, :])
        & (key_places[:, None, :] <= query_places[:, :, None])
        & key_ok[:, None, :]
    )

    queries = jnp.stack([early_queries, late_queries]).reshape(
        2, SPAN, KEY_VALUE_HEADS, QUERY_PER_KV, HEAD_SIZE
    )
    keys = key_blocks[:, :, :key_cols].reshape(2, -1, KEY_VALUE_HEADS, HEAD_SIZE)
    values = key_blocks[:, :, key_cols:].reshape(2, -1, KEY_VALUE_HEADS, HEAD_SIZE)
    scores = (
        jnp.einsum("sqhgd,skhd->shgqk", queries, keys, preferred_element_type=jnp.float32)
        * 0.125
    )
    live = live[:, None, None]
    scores = jnp.where(live, scores, -1e30)
    top = jnp.max(scores, axis=-1, keepdims=True)
    weights = jnp.where(live, jnp.exp(scores - top), 0.0)
    total = jnp.sum(weights, axis=-1)
    summed = jnp.einsum(
        "shgqk,skhd->shgqd",
        weights.astype(jnp.bfloat16),
        values,
        preferred_element_type=jnp.float32,
    )
    outputs = summed / total[..., None]
    outputs = jnp.transpose(outputs, (0, 3, 1, 2, 4)).reshape(2, SPAN, QUERY_HEADS * HEAD_SIZE)
    outputs = outputs.astype(jnp.bfloat16)
    ordered = jnp.where(early_first, outputs, outputs[::-1]).reshape(
        token_count, QUERY_HEADS * HEAD_SIZE
    )
    return ordered[None]


def solution(mesh):
    placed = (P("seq", "ctx", None), P(None, "seq"), P("seq", None), P("seq", None))
    return jax.shard_map(
        body, mesh=mesh, in_specs=placed, out_specs=P("seq", "ctx", None), check_vma=False
    )
```

```python
import jax
import jax.numpy as jnp
from jax import lax
from jax.sharding import PartitionSpec as P
from jax.experimental import pallas as pl
from jax.experimental.pallas import tpu as pltpu

QUERY_HEADS = 16
KEY_VALUE_HEADS = 4
HEAD_SIZE = 64
QUERY_PER_KV = 4
SPAN = 64
DOC_MOST = 1024
WINDOW = DOC_MOST // SPAN


def apply_rotary(value_rows, token_positions):
    token_count = value_rows.shape[0]
    heads = value_rows.reshape(token_count, -1, HEAD_SIZE)
    half = HEAD_SIZE // 2
    freq = 500000.0 ** (-jnp.arange(half, dtype=jnp.float32) * 2.0 / HEAD_SIZE)
    angle = token_positions.astype(jnp.float32)[:, None] * freq[None, :]
    cosine = jnp.cos(angle)[:, None, :]
    sine = jnp.sin(angle)[:, None, :]
    first = heads[..., :half]
    second = heads[..., half:]
    turned = jnp.concatenate(
        [first * cosine - second * sine, second * cosine + first * sine], axis=-1
    )
    return turned.reshape(token_count, -1)


def positions(order_row):
    offsets = jnp.arange(SPAN, dtype=jnp.int32)
    return (order_row[:, None] * SPAN + offsets[None, :]).reshape(-1)


def documents(lengths_row, token_positions):
    ends = jnp.cumsum(lengths_row)
    return jnp.sum((ends[None, :] <= token_positions[..., None]).astype(jnp.int32), axis=-1)


def moved(value, count, pairs):
    pairs = [(s, d) for s, d in pairs if 0 <= s < count and 0 <= d < count]
    if not pairs:
        return jnp.zeros_like(value)
    return lax.ppermute(value, "ctx", pairs)


def chip_of(index, lanes):
    line, core = divmod(index // lanes, 2)
    half, rest = divmod(index % lanes, lanes // 2)
    return line, core, half, rest


def device_of(line, core, half, rest, lanes, lines):
    return (2 * line + core) * lanes + half * (lanes // 2) + rest


def project(rows, weight):
    lines = lax.axis_size("seq") // 2
    lanes = lax.axis_size("ctx")
    total = 2 * lines * lanes
    both = ("seq", "ctx")

    def pairs_for(offset):
        found = []
        for dest in range(total):
            line, core, half, rest = chip_of(dest, lanes)
            level = half * lines + line + offset(core)
            level %= 2 * lines
            found.append((device_of(level % lines, core, level // lines, rest, lanes, lines), dest))
        return found

    def mate_pairs():
        found = []
        for dest in range(total):
            line, core, half, rest = chip_of(dest, lanes)
            found.append((device_of(line, 1 - core, half, rest, lanes, lines), dest))
        return found

    step = [lambda core: 0]
    for shift in range(1, lines):
        if 2 * shift == lines:
            step.append(lambda core, s=shift: s if core == 0 else -s)
        elif 2 * shift < lines:
            step.append(lambda core, s=shift: s)
        else:
            step.append(lambda core, s=shift: s - lines)
    mine = [weight] + [lax.ppermute(weight, both, pairs_for(f)) for f in step[1:]]
    mate = lax.ppermute(jnp.stack(mine), both, mate_pairs())
    parts = [jnp.dot(rows, block, preferred_element_type=jnp.float32) for block in mine]
    parts += [
        jnp.dot(rows, mate[index], preferred_element_type=jnp.float32) for index in range(len(mine))
    ]
    parts = jnp.stack(parts).astype(jnp.bfloat16)
    seq_index = lax.axis_index("seq")
    line, core = seq_index // 2, seq_index % 2
    wanted = jnp.arange(2 * lines, dtype=jnp.int32)
    slot = (wanted // 2 - line) % lines + lines * (wanted % 2 != core).astype(jnp.int32)
    ordered = jnp.take(parts, slot, axis=0)
    return jnp.transpose(ordered, (1, 0, 2)).reshape(rows.shape[0], -1)


def body(tokens, qkv_weight, doc_lengths, span_order):
    rows = tokens[0]
    token_count = rows.shape[0]
    query_key_value = project(rows, qkv_weight)
    lengths_row = doc_lengths[0]
    order_row = span_order[0]
    places_all = positions(order_row)
    my_index = lax.axis_index("ctx")
    devices = lax.axis_size("ctx")
    first_row = my_index * token_count
    token_positions = lax.dynamic_slice_in_dim(places_all, first_row, token_count)
    query_rows = apply_rotary(
        query_key_value[:, : QUERY_HEADS * HEAD_SIZE].astype(jnp.float32), token_positions
    ).astype(jnp.bfloat16)
    key_rows = apply_rotary(
        query_key_value[
            :, QUERY_HEADS * HEAD_SIZE : (QUERY_HEADS + KEY_VALUE_HEADS) * HEAD_SIZE
        ].astype(jnp.float32),
        token_positions,
    ).astype(jnp.bfloat16)
    value_rows = query_key_value[:, (QUERY_HEADS + KEY_VALUE_HEADS) * HEAD_SIZE :]
    key_cols = key_rows.shape[1]
    stacked = jnp.concatenate([key_rows, value_rows], axis=1)

    early_first = order_row[2 * my_index] < devices
    offset = jnp.where(early_first, 0, SPAN).astype(jnp.int32)
    early_rows = lax.dynamic_slice_in_dim(stacked, offset, SPAN, 0)
    late_rows = lax.dynamic_slice_in_dim(stacked, SPAN - offset, SPAN, 0)
    early_queries = lax.dynamic_slice_in_dim(query_rows, offset, SPAN, 0)
    late_queries = lax.dynamic_slice_in_dim(query_rows, SPAN - offset, SPAN, 0)

    count = devices
    up = early_rows[None]
    down = jnp.stack([early_rows, late_rows])[None]
    reach = 1
    while reach < WINDOW:
        up = jnp.concatenate(
            [up, moved(up, count, [(d, d + reach) for d in range(count)])], axis=0
        )
        if 2 * reach < WINDOW:
            got = moved(down, count, [(d, d - reach) for d in range(count)])
        else:
            tail = range(count - reach, count)
            got = jnp.stack(
                [
                    moved(down[:, 0], count, [(d, d - reach) for d in tail]),
                    moved(down[:, 1], count, [(d, d - reach) for d in range(count)]),
                ],
                axis=1,
            )
        down = jnp.concatenate([down, got], axis=0)
        reach *= 2
    up = jnp.concatenate(
        [up, moved(early_rows[None], count, [(d, d + WINDOW) for d in range(count)])], axis=0
    )
    far = moved(late_rows[None], count, [(d, d - WINDOW) for d in range(count)])
    down = jnp.concatenate([down, jnp.stack([jnp.zeros_like(far), far], axis=1)], axis=0)
    early_keys = up.reshape(-1, up.shape[-1])
    around = jnp.concatenate([up, down[:, 0], down[:, 1]], axis=0)
    steps = jnp.arange(WINDOW + 1, dtype=jnp.int32)
    source = 2 * count - 1 - my_index - steps
    pick = jnp.where(
        my_index + steps <= count - 1,
        2 * (WINDOW + 1) + steps,
        jnp.where(source <= my_index, my_index - source, WINDOW + 1 + source - my_index),
    )
    pick = jnp.clip(pick, 0, around.shape[0] - 1)
    late_keys = jnp.take(around, pick, axis=0).reshape(-1, up.shape[-1])
    key_blocks = jnp.stack([early_keys, late_keys])

    steps = jnp.arange(WINDOW + 1, dtype=jnp.int32)
    query_spans = jnp.stack([my_index, 2 * devices - 1 - my_index])
    key_spans = query_spans[:, None] - steps[None, :]
    ramp = jnp.arange(SPAN, dtype=jnp.int32)
    key_places = (key_spans[:, :, None] * SPAN + ramp).reshape(2, -1)
    key_ok = jnp.repeat(key_spans >= 0, SPAN, axis=1)
    query_places = query_spans[:, None] * SPAN + ramp[None, :]
    key_docs = documents(lengths_row, key_places)
    query_docs = documents(lengths_row, query_places)
    live = (
        (query_docs[:, :, None] == key_docs[:, None, :])
        & (key_places[:, None, :] <= query_places[:, :, None])
        & key_ok[:, None, :]
    )

    key_docs = jnp.where(key_ok, key_docs, -1)
    return attend(
        offset.reshape(1),
        query_rows,
        early_keys,
        late_keys,
        query_places[:, :, None],
        query_docs[:, :, None],
        key_places[:, None, :],
        key_docs[:, None, :],
    )[None]


def attend_kernel(offset_ref, q_ref, early_ref, late_ref, qpos_ref, qdoc_ref, kpos_ref, kdoc_ref, o_ref):
    offset = pl.multiple_of(offset_ref[0], SPAN)
    for span, kv_ref in ((0, early_ref), (1, late_ref)):
        row = offset if span == 0 else SPAN - offset
        row = pl.multiple_of(row, SPAN)
        live = (qdoc_ref[span] == kdoc_ref[span]) & (kpos_ref[span] <= qpos_ref[span])
        for group in range(KEY_VALUE_HEADS):
            key = kv_ref[:, group * HEAD_SIZE : (group + 1) * HEAD_SIZE]
            base = KEY_VALUE_HEADS * HEAD_SIZE + group * HEAD_SIZE
            value = kv_ref[:, base : base + HEAD_SIZE]
            for member in range(QUERY_PER_KV):
                head = group * QUERY_PER_KV + member
                cols = slice(head * HEAD_SIZE, (head + 1) * HEAD_SIZE)
                query = q_ref[pl.ds(row, SPAN), cols]
                scores = lax.dot_general(
                    query, key, (((1,), (1,)), ((), ())), preferred_element_type=jnp.float32
                ) * 0.125
                scores = jnp.where(live, scores, -1e30)
                top = jnp.max(scores, axis=1, keepdims=True)
                weights = jnp.where(live, jnp.exp(scores - top), 0.0)
                total = jnp.sum(weights, axis=1, keepdims=True)
                summed = jnp.dot(
                    weights.astype(jnp.bfloat16), value, preferred_element_type=jnp.float32
                )
                o_ref[pl.ds(row, SPAN), cols] = (summed / total).astype(o_ref.dtype)


def attend(offset, query_rows, early_keys, late_keys, qpos, qdoc, kpos, kdoc):
    vmem = pl.BlockSpec(memory_space=pltpu.VMEM)
    return pl.pallas_call(
        attend_kernel,
        out_shape=jax.ShapeDtypeStruct(query_rows.shape, query_rows.dtype),
        in_specs=[pl.BlockSpec(memory_space=pltpu.SMEM)] + [vmem] * 7,
        out_specs=vmem,
    )(offset, query_rows, early_keys, late_keys, qpos, qdoc, kpos, kdoc)


def solution(mesh):
    placed = (P("seq", "ctx", None), P(None, "seq"), P("seq", None), P("seq", None))
    return jax.shard_map(
        body, mesh=mesh, in_specs=placed, out_specs=P("seq", "ctx", None), check_vma=False
    )
```

```python
import jax
import jax.numpy as jnp
from jax import lax
from jax.sharding import PartitionSpec as P
from jax.experimental import pallas as pl
from jax.experimental.pallas import tpu as pltpu

QUERY_HEADS = 16
KEY_VALUE_HEADS = 4
HEAD_SIZE = 64
QUERY_PER_KV = 4
SPAN = 64
DOC_MOST = 1024
WINDOW = DOC_MOST // SPAN


def apply_rotary(value_rows, token_positions):
    token_count = value_rows.shape[0]
    heads = value_rows.reshape(token_count, -1, HEAD_SIZE)
    half = HEAD_SIZE // 2
    freq = 500000.0 ** (-jnp.arange(half, dtype=jnp.float32) * 2.0 / HEAD_SIZE)
    angle = token_positions.astype(jnp.float32)[:, None] * freq[None, :]
    cosine = jnp.cos(angle)[:, None, :]
    sine = jnp.sin(angle)[:, None, :]
    first = heads[..., :half]
    second = heads[..., half:]
    turned = jnp.concatenate(
        [first * cosine - second * sine, second * cosine + first * sine], axis=-1
    )
    return turned.reshape(token_count, -1)


def positions(order_row):
    offsets = jnp.arange(SPAN, dtype=jnp.int32)
    return (order_row[:, None] * SPAN + offsets[None, :]).reshape(-1)


def documents(lengths_row, token_positions):
    ends = jnp.cumsum(lengths_row)
    return jnp.sum((ends[None, :] <= token_positions[..., None]).astype(jnp.int32), axis=-1)


def moved(value, count, pairs):
    pairs = [(s, d) for s, d in pairs if 0 <= s < count and 0 <= d < count]
    if not pairs:
        return jnp.zeros_like(value)
    return lax.ppermute(value, "ctx", pairs)


def chip_of(index, lanes):
    line, core = divmod(index // lanes, 2)
    half, rest = divmod(index % lanes, lanes // 2)
    return line, core, half, rest


def device_of(line, core, half, rest, lanes, lines):
    return (2 * line + core) * lanes + half * (lanes // 2) + rest


def project(rows, weight):
    lines = lax.axis_size("seq") // 2
    lanes = lax.axis_size("ctx")
    total = 2 * lines * lanes
    both = ("seq", "ctx")

    def pairs_for(offset):
        found = []
        for dest in range(total):
            line, core, half, rest = chip_of(dest, lanes)
            level = half * lines + line + offset(core)
            level %= 2 * lines
            found.append((device_of(level % lines, core, level // lines, rest, lanes, lines), dest))
        return found

    def mate_pairs():
        found = []
        for dest in range(total):
            line, core, half, rest = chip_of(dest, lanes)
            found.append((device_of(line, 1 - core, half, rest, lanes, lines), dest))
        return found

    step = [lambda core: 0]
    for shift in range(1, lines):
        if 2 * shift == lines:
            step.append(lambda core, s=shift: s if core == 0 else -s)
        elif 2 * shift < lines:
            step.append(lambda core, s=shift: s)
        else:
            step.append(lambda core, s=shift: s - lines)
    mine = [weight] + [lax.ppermute(weight, both, pairs_for(f)) for f in step[1:]]
    mate = lax.ppermute(jnp.stack(mine), both, mate_pairs())
    parts = [jnp.dot(rows, block, preferred_element_type=jnp.float32) for block in mine]
    parts += [
        jnp.dot(rows, mate[index], preferred_element_type=jnp.float32) for index in range(len(mine))
    ]
    parts = jnp.stack(parts).astype(jnp.bfloat16)
    seq_index = lax.axis_index("seq")
    line, core = seq_index // 2, seq_index % 2
    wanted = jnp.arange(2 * lines, dtype=jnp.int32)
    slot = (wanted // 2 - line) % lines + lines * (wanted % 2 != core).astype(jnp.int32)
    ordered = jnp.take(parts, slot, axis=0)
    return jnp.transpose(ordered, (1, 0, 2)).reshape(rows.shape[0], -1)


def body(tokens, qkv_weight, doc_lengths, span_order):
    rows = tokens[0]
    token_count = rows.shape[0]
    query_key_value = project(rows, qkv_weight)
    lengths_row = doc_lengths[0]
    order_row = span_order[0]
    places_all = positions(order_row)
    my_index = lax.axis_index("ctx")
    devices = lax.axis_size("ctx")
    first_row = my_index * token_count
    token_positions = lax.dynamic_slice_in_dim(places_all, first_row, token_count)
    query_rows = apply_rotary(
        query_key_value[:, : QUERY_HEADS * HEAD_SIZE].astype(jnp.float32), token_positions
    ).astype(jnp.bfloat16)
    key_rows = apply_rotary(
        query_key_value[
            :, QUERY_HEADS * HEAD_SIZE : (QUERY_HEADS + KEY_VALUE_HEADS) * HEAD_SIZE
        ].astype(jnp.float32),
        token_positions,
    ).astype(jnp.bfloat16)
    value_rows = query_key_value[:, (QUERY_HEADS + KEY_VALUE_HEADS) * HEAD_SIZE :]
    key_cols = key_rows.shape[1]
    stacked = jnp.concatenate([key_rows, value_rows], axis=1)

    early_first = order_row[2 * my_index] < devices
    offset = jnp.where(early_first, 0, SPAN).astype(jnp.int32)
    early_rows = lax.dynamic_slice_in_dim(stacked, offset, SPAN, 0)
    late_rows = lax.dynamic_slice_in_dim(stacked, SPAN - offset, SPAN, 0)
    early_queries = lax.dynamic_slice_in_dim(query_rows, offset, SPAN, 0)
    late_queries = lax.dynamic_slice_in_dim(query_rows, SPAN - offset, SPAN, 0)

    count = devices
    up = early_rows[None]
    down = jnp.stack([early_rows, late_rows])[None]
    reach = 1
    while reach < WINDOW:
        up = jnp.concatenate(
            [up, moved(up, count, [(d, d + reach) for d in range(count)])], axis=0
        )
        if 2 * reach < WINDOW:
            got = moved(down, count, [(d, d - reach) for d in range(count)])
        else:
            tail = range(count - reach, count)
            got = jnp.stack(
                [
                    moved(down[:, 0], count, [(d, d - reach) for d in tail]),
                    moved(down[:, 1], count, [(d, d - reach) for d in range(count)]),
                ],
                axis=1,
            )
        down = jnp.concatenate([down, got], axis=0)
        reach *= 2
    up = jnp.concatenate(
        [up, moved(early_rows[None], count, [(d, d + WINDOW) for d in range(count)])], axis=0
    )
    far = moved(late_rows[None], count, [(d, d - WINDOW) for d in range(count)])
    down = jnp.concatenate([down, jnp.stack([jnp.zeros_like(far), far], axis=1)], axis=0)
    early_keys = up.reshape(-1, up.shape[-1])
    around = jnp.concatenate([up, down[:, 0], down[:, 1]], axis=0)
    steps = jnp.arange(WINDOW + 1, dtype=jnp.int32)
    source = 2 * count - 1 - my_index - steps
    pick = jnp.where(
        my_index + steps <= count - 1,
        2 * (WINDOW + 1) + steps,
        jnp.where(source <= my_index, my_index - source, WINDOW + 1 + source - my_index),
    )
    pick = jnp.clip(pick, 0, around.shape[0] - 1)
    late_keys = jnp.take(around, pick, axis=0).reshape(-1, up.shape[-1])
    key_blocks = jnp.stack([early_keys, late_keys])

    steps = jnp.arange(WINDOW + 1, dtype=jnp.int32)
    query_spans = jnp.stack([my_index, 2 * devices - 1 - my_index])
    key_spans = query_spans[:, None] - steps[None, :]
    ramp = jnp.arange(SPAN, dtype=jnp.int32)
    key_places = (key_spans[:, :, None] * SPAN + ramp).reshape(2, -1)
    key_ok = jnp.repeat(key_spans >= 0, SPAN, axis=1)
    query_places = query_spans[:, None] * SPAN + ramp[None, :]
    key_docs = documents(lengths_row, key_places)
    query_docs = documents(lengths_row, query_places)
    live = (
        (query_docs[:, :, None] == key_docs[:, None, :])
        & (key_places[:, None, :] <= query_places[:, :, None])
        & key_ok[:, None, :]
    )

    key_docs = jnp.where(key_ok, key_docs, -1)
    pad = CHUNK - key_places.shape[1] % CHUNK
    key_places = jnp.pad(key_places, ((0, 0), (0, pad)))
    key_docs = jnp.pad(key_docs, ((0, 0), (0, pad)), constant_values=-1)
    early_keys = jnp.pad(early_keys, ((0, pad), (0, 0)))
    late_keys = jnp.pad(late_keys, ((0, pad), (0, 0)))
    ends = jnp.cumsum(lengths_row)
    first = query_spans * SPAN
    opening = jnp.max(jnp.where(ends[None, :] <= first[:, None], ends[None, :], 0), axis=1)
    reach_back = query_spans - opening // SPAN
    chunks = jnp.clip(reach_back // (CHUNK // SPAN) + 1, 1, key_places.shape[1] // CHUNK)
    return attend(
        jnp.concatenate([offset.reshape(1), chunks.astype(jnp.int32)]),
        query_rows,
        early_keys,
        late_keys,
        query_places[:, :, None],
        query_docs[:, :, None],
        key_places[:, None, :],
        key_docs[:, None, :],
    )[None]


CHUNK = 128


def attend_kernel(meta_ref, q_ref, early_ref, late_ref, qpos_ref, qdoc_ref, kpos_ref, kdoc_ref, o_ref):
    offset = pl.multiple_of(meta_ref[0], SPAN)
    rows = QUERY_PER_KV * SPAN
    for span, kv_ref in ((0, early_ref), (1, late_ref)):
        row = offset if span == 0 else SPAN - offset
        row = pl.multiple_of(row, SPAN)
        count = meta_ref[1 + span]
        qpos = qpos_ref[span]
        qdoc = qdoc_ref[span]

        def live_of(start):
            kpos = kpos_ref[span, :, pl.ds(start, CHUNK)]
            kdoc = kdoc_ref[span, :, pl.ds(start, CHUNK)]
            live = (qdoc == kdoc) & (kpos <= qpos)
            return jnp.concatenate([live] * QUERY_PER_KV, axis=0)

        for group in range(KEY_VALUE_HEADS):
            heads = range(group * QUERY_PER_KV, (group + 1) * QUERY_PER_KV)
            query = jnp.concatenate(
                [q_ref[pl.ds(row, SPAN), head * HEAD_SIZE : (head + 1) * HEAD_SIZE] for head in heads],
                axis=0,
            )
            key_cols = slice(group * HEAD_SIZE, (group + 1) * HEAD_SIZE)
            base = KEY_VALUE_HEADS * HEAD_SIZE + group * HEAD_SIZE

            def scores_of(index):
                start = pl.multiple_of(index * CHUNK, CHUNK)
                key = kv_ref[pl.ds(start, CHUNK), key_cols]
                scores = lax.dot_general(
                    query, key, (((1,), (1,)), ((), ())), preferred_element_type=jnp.float32
                ) * 0.125
                return jnp.where(live_of(start), scores, -1e30), start

            def find_top(index, top):
                scores, _ = scores_of(index)
                return jnp.maximum(top, jnp.max(scores, axis=1, keepdims=True))

            top = lax.fori_loop(0, count, find_top, jnp.full((rows, 1), -1e30, jnp.float32))

            def gather(index, carry):
                total, summed = carry
                scores, start = scores_of(index)
                weights = jnp.exp(scores - top)
                value = kv_ref[pl.ds(start, CHUNK), base : base + HEAD_SIZE]
                total = total + jnp.sum(weights, axis=1, keepdims=True)
                summed = summed + jnp.dot(
                    weights.astype(jnp.bfloat16), value, preferred_element_type=jnp.float32
                )
                return total, summed

            total, summed = lax.fori_loop(
                0,
                count,
                gather,
                (jnp.zeros((rows, 1), jnp.float32), jnp.zeros((rows, HEAD_SIZE), jnp.float32)),
            )
            result = (summed / total).astype(o_ref.dtype)
            for member, head in enumerate(heads):
                o_ref[pl.ds(row, SPAN), head * HEAD_SIZE : (head + 1) * HEAD_SIZE] = result[
                    member * SPAN : (member + 1) * SPAN
                ]


def attend(meta, query_rows, early_keys, late_keys, qpos, qdoc, kpos, kdoc):
    vmem = pl.BlockSpec(memory_space=pltpu.VMEM)
    return pl.pallas_call(
        attend_kernel,
        out_shape=jax.ShapeDtypeStruct(query_rows.shape, query_rows.dtype),
        in_specs=[pl.BlockSpec(memory_space=pltpu.SMEM)] + [vmem] * 7,
        out_specs=vmem,
    )(meta, query_rows, early_keys, late_keys, qpos, qdoc, kpos, kdoc)

def solution(mesh):
    placed = (P("seq", "ctx", None), P(None, "seq"), P("seq", None), P("seq", None))
    return jax.shard_map(
        body, mesh=mesh, in_specs=placed, out_specs=P("seq", "ctx", None), check_vma=False
    )
```

```python
import jax
import jax.numpy as jnp
from jax import lax
from jax.sharding import PartitionSpec as P
from jax.experimental import pallas as pl
from jax.experimental.pallas import tpu as pltpu

QUERY_HEADS = 16
KEY_VALUE_HEADS = 4
HEAD_SIZE = 64
QUERY_PER_KV = 4
SPAN = 64
DOC_MOST = 1024
WINDOW = DOC_MOST // SPAN


def apply_rotary(value_rows, token_positions):
    token_count = value_rows.shape[0]
    heads = value_rows.reshape(token_count, -1, HEAD_SIZE)
    half = HEAD_SIZE // 2
    freq = 500000.0 ** (-jnp.arange(half, dtype=jnp.float32) * 2.0 / HEAD_SIZE)
    angle = token_positions.astype(jnp.float32)[:, None] * freq[None, :]
    cosine = jnp.cos(angle)[:, None, :]
    sine = jnp.sin(angle)[:, None, :]
    first = heads[..., :half]
    second = heads[..., half:]
    turned = jnp.concatenate(
        [first * cosine - second * sine, second * cosine + first * sine], axis=-1
    )
    return turned.reshape(token_count, -1)


def positions(order_row):
    offsets = jnp.arange(SPAN, dtype=jnp.int32)
    return (order_row[:, None] * SPAN + offsets[None, :]).reshape(-1)


def documents(lengths_row, token_positions):
    ends = jnp.cumsum(lengths_row)
    return jnp.sum((ends[None, :] <= token_positions[..., None]).astype(jnp.int32), axis=-1)


def moved(value, count, pairs):
    pairs = [(s, d) for s, d in pairs if 0 <= s < count and 0 <= d < count]
    if not pairs:
        return jnp.zeros_like(value)
    return lax.ppermute(value, "ctx", pairs)


def chip_of(index, lanes):
    line, core = divmod(index // lanes, 2)
    half, rest = divmod(index % lanes, lanes // 2)
    return line, core, half, rest


def device_of(line, core, half, rest, lanes, lines):
    return (2 * line + core) * lanes + half * (lanes // 2) + rest


def project(rows, weight):
    lines = lax.axis_size("seq") // 2
    lanes = lax.axis_size("ctx")
    total = 2 * lines * lanes
    both = ("seq", "ctx")

    def pairs_for(offset):
        found = []
        for dest in range(total):
            line, core, half, rest = chip_of(dest, lanes)
            level = half * lines + line + offset(core)
            level %= 2 * lines
            found.append((device_of(level % lines, core, level // lines, rest, lanes, lines), dest))
        return found

    def mate_pairs():
        found = []
        for dest in range(total):
            line, core, half, rest = chip_of(dest, lanes)
            found.append((device_of(line, 1 - core, half, rest, lanes, lines), dest))
        return found

    step = [lambda core: 0]
    for shift in range(1, lines):
        if 2 * shift == lines:
            step.append(lambda core, s=shift: s if core == 0 else -s)
        elif 2 * shift < lines:
            step.append(lambda core, s=shift: s)
        else:
            step.append(lambda core, s=shift: s - lines)
    mine = [weight] + [lax.ppermute(weight, both, pairs_for(f)) for f in step[1:]]
    mate = lax.ppermute(jnp.stack(mine), both, mate_pairs())
    parts = [jnp.dot(rows, block, preferred_element_type=jnp.float32) for block in mine]
    parts += [
        jnp.dot(rows, mate[index], preferred_element_type=jnp.float32) for index in range(len(mine))
    ]
    parts = jnp.stack(parts).astype(jnp.bfloat16)
    seq_index = lax.axis_index("seq")
    line, core = seq_index // 2, seq_index % 2
    wanted = jnp.arange(2 * lines, dtype=jnp.int32)
    slot = (wanted // 2 - line) % lines + lines * (wanted % 2 != core).astype(jnp.int32)
    ordered = jnp.take(parts, slot, axis=0)
    return jnp.transpose(ordered, (1, 0, 2)).reshape(rows.shape[0], -1)


def body(tokens, qkv_weight, doc_lengths, span_order):
    rows = tokens[0]
    token_count = rows.shape[0]
    query_key_value = project(rows, qkv_weight)
    lengths_row = doc_lengths[0]
    order_row = span_order[0]
    places_all = positions(order_row)
    my_index = lax.axis_index("ctx")
    devices = lax.axis_size("ctx")
    first_row = my_index * token_count
    token_positions = lax.dynamic_slice_in_dim(places_all, first_row, token_count)
    query_rows = apply_rotary(
        query_key_value[:, : QUERY_HEADS * HEAD_SIZE].astype(jnp.float32), token_positions
    ).astype(jnp.bfloat16)
    key_rows = apply_rotary(
        query_key_value[
            :, QUERY_HEADS * HEAD_SIZE : (QUERY_HEADS + KEY_VALUE_HEADS) * HEAD_SIZE
        ].astype(jnp.float32),
        token_positions,
    ).astype(jnp.bfloat16)
    value_rows = query_key_value[:, (QUERY_HEADS + KEY_VALUE_HEADS) * HEAD_SIZE :]
    key_cols = key_rows.shape[1]
    stacked = jnp.concatenate([key_rows, value_rows], axis=1)

    early_first = order_row[2 * my_index] < devices
    offset = jnp.where(early_first, 0, SPAN).astype(jnp.int32)
    early_rows = lax.dynamic_slice_in_dim(stacked, offset, SPAN, 0)
    late_rows = lax.dynamic_slice_in_dim(stacked, SPAN - offset, SPAN, 0)
    early_queries = lax.dynamic_slice_in_dim(query_rows, offset, SPAN, 0)
    late_queries = lax.dynamic_slice_in_dim(query_rows, SPAN - offset, SPAN, 0)

    count = devices
    up = early_rows[None]
    down = jnp.stack([early_rows, late_rows])[None]
    reach = 1
    lone_early, lone_late = early_rows[None], late_rows[None]
    while reach < WINDOW:
        if 2 * reach == WINDOW:
            lone_early, lone_late, up, down = lax.optimization_barrier(
                (lone_early, lone_late, up, down)
            )
        up = jnp.concatenate(
            [up, moved(up, count, [(d, d + reach) for d in range(count)])], axis=0
        )
        if 2 * reach < WINDOW:
            got = moved(down, count, [(d, d - reach) for d in range(count)])
        else:
            tail = range(count - reach, count)
            got = jnp.stack(
                [
                    moved(down[:, 0], count, [(d, d - reach) for d in tail]),
                    moved(down[:, 1], count, [(d, d - reach) for d in range(count)]),
                ],
                axis=1,
            )
        down = jnp.concatenate([down, got], axis=0)
        reach *= 2
    up = jnp.concatenate(
        [up, moved(lone_early, count, [(d, d + WINDOW) for d in range(count)])], axis=0
    )
    far = moved(lone_late, count, [(d, d - WINDOW) for d in range(count)])
    down = jnp.concatenate([down, jnp.stack([jnp.zeros_like(far), far], axis=1)], axis=0)
    early_keys = up.reshape(-1, up.shape[-1])
    around = jnp.concatenate([up, down[:, 0], down[:, 1]], axis=0)
    steps = jnp.arange(WINDOW + 1, dtype=jnp.int32)
    source = 2 * count - 1 - my_index - steps
    pick = jnp.where(
        my_index + steps <= count - 1,
        2 * (WINDOW + 1) + steps,
        jnp.where(source <= my_index, my_index - source, WINDOW + 1 + source - my_index),
    )
    pick = jnp.clip(pick, 0, around.shape[0] - 1)
    late_keys = jnp.take(around, pick, axis=0).reshape(-1, up.shape[-1])
    key_blocks = jnp.stack([early_keys, late_keys])

    steps = jnp.arange(WINDOW + 1, dtype=jnp.int32)
    query_spans = jnp.stack([my_index, 2 * devices - 1 - my_index])
    key_spans = query_spans[:, None] - steps[None, :]
    ramp = jnp.arange(SPAN, dtype=jnp.int32)
    key_places = (key_spans[:, :, None] * SPAN + ramp).reshape(2, -1)
    key_ok = jnp.repeat(key_spans >= 0, SPAN, axis=1)
    query_places = query_spans[:, None] * SPAN + ramp[None, :]
    key_docs = documents(lengths_row, key_places)
    query_docs = documents(lengths_row, query_places)
    live = (
        (query_docs[:, :, None] == key_docs[:, None, :])
        & (key_places[:, None, :] <= query_places[:, :, None])
        & key_ok[:, None, :]
    )

    key_docs = jnp.where(key_ok, key_docs, -1)
    return attend(
        offset.reshape(1),
        query_rows,
        early_keys,
        late_keys,
        query_places[:, :, None],
        query_docs[:, :, None],
        key_places[:, None, :],
        key_docs[:, None, :],
    )[None]


def attend_kernel(offset_ref, q_ref, early_ref, late_ref, qpos_ref, qdoc_ref, kpos_ref, kdoc_ref, o_ref):
    offset = pl.multiple_of(offset_ref[0], SPAN)
    for span, kv_ref in ((0, early_ref), (1, late_ref)):
        row = offset if span == 0 else SPAN - offset
        row = pl.multiple_of(row, SPAN)
        live = (qdoc_ref[span] == kdoc_ref[span]) & (kpos_ref[span] <= qpos_ref[span])
        for group in range(KEY_VALUE_HEADS):
            key = kv_ref[:, group * HEAD_SIZE : (group + 1) * HEAD_SIZE]
            base = KEY_VALUE_HEADS * HEAD_SIZE + group * HEAD_SIZE
            value = kv_ref[:, base : base + HEAD_SIZE]
            for member in range(QUERY_PER_KV):
                head = group * QUERY_PER_KV + member
                cols = slice(head * HEAD_SIZE, (head + 1) * HEAD_SIZE)
                query = q_ref[pl.ds(row, SPAN), cols]
                scores = lax.dot_general(
                    query, key, (((1,), (1,)), ((), ())), preferred_element_type=jnp.float32
                ) * 0.125
                scores = jnp.where(live, scores, -1e30)
                top = jnp.max(scores, axis=1, keepdims=True)
                weights = jnp.where(live, jnp.exp(scores - top), 0.0)
                total = jnp.sum(weights, axis=1, keepdims=True)
                summed = jnp.dot(
                    weights.astype(jnp.bfloat16), value, preferred_element_type=jnp.float32
                )
                o_ref[pl.ds(row, SPAN), cols] = (summed / total).astype(o_ref.dtype)


def attend(offset, query_rows, early_keys, late_keys, qpos, qdoc, kpos, kdoc):
    vmem = pl.BlockSpec(memory_space=pltpu.VMEM)
    return pl.pallas_call(
        attend_kernel,
        out_shape=jax.ShapeDtypeStruct(query_rows.shape, query_rows.dtype),
        in_specs=[pl.BlockSpec(memory_space=pltpu.SMEM)] + [vmem] * 7,
        out_specs=vmem,
    )(offset, query_rows, early_keys, late_keys, qpos, qdoc, kpos, kdoc)


def solution(mesh):
    placed = (P("seq", "ctx", None), P(None, "seq"), P("seq", None), P("seq", None))
    return jax.shard_map(
        body, mesh=mesh, in_specs=placed, out_specs=P("seq", "ctx", None), check_vma=False
    )
```

```python
import jax
import jax.numpy as jnp
from jax import lax
from jax.sharding import PartitionSpec as P
from jax.experimental import pallas as pl
from jax.experimental.pallas import tpu as pltpu

QUERY_HEADS = 16
KEY_VALUE_HEADS = 4
HEAD_SIZE = 64
QUERY_PER_KV = 4
SPAN = 64
DOC_MOST = 1024
WINDOW = DOC_MOST // SPAN


def apply_rotary(value_rows, token_positions):
    token_count = value_rows.shape[0]
    heads = value_rows.reshape(token_count, -1, HEAD_SIZE)
    half = HEAD_SIZE // 2
    freq = 500000.0 ** (-jnp.arange(half, dtype=jnp.float32) * 2.0 / HEAD_SIZE)
    angle = token_positions.astype(jnp.float32)[:, None] * freq[None, :]
    cosine = jnp.cos(angle)[:, None, :]
    sine = jnp.sin(angle)[:, None, :]
    first = heads[..., :half]
    second = heads[..., half:]
    turned = jnp.concatenate(
        [first * cosine - second * sine, second * cosine + first * sine], axis=-1
    )
    return turned.reshape(token_count, -1)


def positions(order_row):
    offsets = jnp.arange(SPAN, dtype=jnp.int32)
    return (order_row[:, None] * SPAN + offsets[None, :]).reshape(-1)


def documents(lengths_row, token_positions):
    ends = jnp.cumsum(lengths_row)
    return jnp.sum((ends[None, :] <= token_positions[..., None]).astype(jnp.int32), axis=-1)


def moved(value, count, pairs):
    pairs = [(s, d) for s, d in pairs if 0 <= s < count and 0 <= d < count]
    if not pairs:
        return jnp.zeros_like(value)
    return lax.ppermute(value, "ctx", pairs)


def chip_of(index, lanes):
    line, core = divmod(index // lanes, 2)
    half, rest = divmod(index % lanes, lanes // 2)
    return line, core, half, rest


def device_of(line, core, half, rest, lanes, lines):
    return (2 * line + core) * lanes + half * (lanes // 2) + rest


def project(rows, weight):
    lines = lax.axis_size("seq") // 2
    lanes = lax.axis_size("ctx")
    total = 2 * lines * lanes
    both = ("seq", "ctx")

    def pairs_for(offset):
        found = []
        for dest in range(total):
            line, core, half, rest = chip_of(dest, lanes)
            level = half * lines + line + offset(core)
            level %= 2 * lines
            found.append((device_of(level % lines, core, level // lines, rest, lanes, lines), dest))
        return found

    def mate_pairs():
        found = []
        for dest in range(total):
            line, core, half, rest = chip_of(dest, lanes)
            found.append((device_of(line, 1 - core, half, rest, lanes, lines), dest))
        return found

    step = [lambda core: 0]
    for shift in range(1, lines):
        if 2 * shift == lines:
            step.append(lambda core, s=shift: s if core == 0 else -s)
        elif 2 * shift < lines:
            step.append(lambda core, s=shift: s)
        else:
            step.append(lambda core, s=shift: s - lines)
    mine = [weight] + [lax.ppermute(weight, both, pairs_for(f)) for f in step[1:]]
    mate = lax.ppermute(jnp.stack(mine), both, mate_pairs())
    parts = [jnp.dot(rows, block, preferred_element_type=jnp.float32) for block in mine]
    parts += [
        jnp.dot(rows, mate[index], preferred_element_type=jnp.float32) for index in range(len(mine))
    ]
    parts = jnp.stack(parts).astype(jnp.bfloat16)
    seq_index = lax.axis_index("seq")
    line, core = seq_index // 2, seq_index % 2
    wanted = jnp.arange(2 * lines, dtype=jnp.int32)
    slot = (wanted // 2 - line) % lines + lines * (wanted % 2 != core).astype(jnp.int32)
    ordered = jnp.take(parts, slot, axis=0)
    return jnp.transpose(ordered, (1, 0, 2)).reshape(rows.shape[0], -1)


def body(tokens, qkv_weight, doc_lengths, span_order):
    rows = tokens[0]
    token_count = rows.shape[0]
    query_key_value = project(rows, qkv_weight)
    lengths_row = doc_lengths[0]
    order_row = span_order[0]
    places_all = positions(order_row)
    my_index = lax.axis_index("ctx")
    devices = lax.axis_size("ctx")
    first_row = my_index * token_count
    token_positions = lax.dynamic_slice_in_dim(places_all, first_row, token_count)
    query_rows = apply_rotary(
        query_key_value[:, : QUERY_HEADS * HEAD_SIZE].astype(jnp.float32), token_positions
    ).astype(jnp.bfloat16)
    key_rows = apply_rotary(
        query_key_value[
            :, QUERY_HEADS * HEAD_SIZE : (QUERY_HEADS + KEY_VALUE_HEADS) * HEAD_SIZE
        ].astype(jnp.float32),
        token_positions,
    ).astype(jnp.bfloat16)
    value_rows = query_key_value[:, (QUERY_HEADS + KEY_VALUE_HEADS) * HEAD_SIZE :]
    key_cols = key_rows.shape[1]
    stacked = jnp.concatenate([key_rows, value_rows], axis=1)

    early_first = order_row[2 * my_index] < devices
    offset = jnp.where(early_first, 0, SPAN).astype(jnp.int32)
    early_rows = lax.dynamic_slice_in_dim(stacked, offset, SPAN, 0)
    late_rows = lax.dynamic_slice_in_dim(stacked, SPAN - offset, SPAN, 0)
    early_queries = lax.dynamic_slice_in_dim(query_rows, offset, SPAN, 0)
    late_queries = lax.dynamic_slice_in_dim(query_rows, SPAN - offset, SPAN, 0)

    count = devices
    up = early_rows[None]
    down = jnp.stack([early_rows, late_rows])[None]
    reach = 1
    while reach < WINDOW:
        up = jnp.concatenate(
            [up, moved(up, count, [(d, d + reach) for d in range(count)])], axis=0
        )
        if 2 * reach < WINDOW:
            got = moved(down, count, [(d, d - reach) for d in range(count)])
        else:
            tail = range(count - reach, count)
            got = jnp.stack(
                [
                    moved(down[:, 0], count, [(d, d - reach) for d in tail]),
                    moved(down[:, 1], count, [(d, d - reach) for d in range(count)]),
                ],
                axis=1,
            )
        down = jnp.concatenate([down, got], axis=0)
        reach *= 2
    up = jnp.concatenate(
        [up, moved(early_rows[None], count, [(d, d + WINDOW) for d in range(count)])], axis=0
    )
    far = moved(late_rows[None], count, [(d, d - WINDOW) for d in range(count)])
    down = jnp.concatenate([down, jnp.stack([jnp.zeros_like(far), far], axis=1)], axis=0)
    early_keys = up.reshape(-1, up.shape[-1])
    around = jnp.concatenate([up, down[:, 0], down[:, 1]], axis=0)
    steps = jnp.arange(WINDOW + 1, dtype=jnp.int32)
    source = 2 * count - 1 - my_index - steps
    pick = jnp.where(
        my_index + steps <= count - 1,
        2 * (WINDOW + 1) + steps,
        jnp.where(source <= my_index, my_index - source, WINDOW + 1 + source - my_index),
    )
    pick = jnp.clip(pick, 0, around.shape[0] - 1)
    late_keys = jnp.take(around, pick, axis=0).reshape(-1, up.shape[-1])
    key_blocks = jnp.stack([early_keys, late_keys])

    steps = jnp.arange(WINDOW + 1, dtype=jnp.int32)
    query_spans = jnp.stack([my_index, 2 * devices - 1 - my_index])
    key_spans = query_spans[:, None] - steps[None, :]
    ramp = jnp.arange(SPAN, dtype=jnp.int32)
    key_places = (key_spans[:, :, None] * SPAN + ramp).reshape(2, -1)
    key_ok = jnp.repeat(key_spans >= 0, SPAN, axis=1)
    query_places = query_spans[:, None] * SPAN + ramp[None, :]
    key_docs = documents(lengths_row, key_places)
    query_docs = documents(lengths_row, query_places)
    live = (
        (query_docs[:, :, None] == key_docs[:, None, :])
        & (key_places[:, None, :] <= query_places[:, :, None])
        & key_ok[:, None, :]
    )

    key_docs = jnp.where(key_ok, key_docs, -1)
    return attend(
        offset.reshape(1),
        query_rows,
        early_keys,
        late_keys,
        query_places[:, :, None],
        query_docs[:, :, None],
        key_places[:, None, :],
        key_docs[:, None, :],
    )[None]


def attend_kernel(offset_ref, q_ref, early_ref, late_ref, qpos_ref, qdoc_ref, kpos_ref, kdoc_ref, o_ref):
    offset = pl.multiple_of(offset_ref[0], SPAN)
    for span, kv_ref in ((0, early_ref), (1, late_ref)):
        row = offset if span == 0 else SPAN - offset
        row = pl.multiple_of(row, SPAN)
        live = (qdoc_ref[span] == kdoc_ref[span]) & (kpos_ref[span] <= qpos_ref[span])
        live = jnp.concatenate([live] * QUERY_PER_KV, axis=0)
        for group in range(KEY_VALUE_HEADS):
            key = kv_ref[:, group * HEAD_SIZE : (group + 1) * HEAD_SIZE]
            base = KEY_VALUE_HEADS * HEAD_SIZE + group * HEAD_SIZE
            value = kv_ref[:, base : base + HEAD_SIZE]
            heads = range(group * QUERY_PER_KV, (group + 1) * QUERY_PER_KV)
            query = jnp.concatenate(
                [q_ref[pl.ds(row, SPAN), head * HEAD_SIZE : (head + 1) * HEAD_SIZE] for head in heads],
                axis=0,
            )
            scores = lax.dot_general(
                query, key, (((1,), (1,)), ((), ())), preferred_element_type=jnp.float32
            ) * 0.125
            scores = jnp.where(live, scores, -1e30)
            top = jnp.max(scores, axis=1, keepdims=True)
            weights = jnp.exp(scores - top)
            total = jnp.sum(weights, axis=1, keepdims=True)
            summed = jnp.dot(weights.astype(jnp.bfloat16), value, preferred_element_type=jnp.float32)
            result = (summed / total).astype(o_ref.dtype)
            for member, head in enumerate(heads):
                o_ref[pl.ds(row, SPAN), head * HEAD_SIZE : (head + 1) * HEAD_SIZE] = result[
                    member * SPAN : (member + 1) * SPAN
                ]


def attend(offset, query_rows, early_keys, late_keys, qpos, qdoc, kpos, kdoc):
    vmem = pl.BlockSpec(memory_space=pltpu.VMEM)
    return pl.pallas_call(
        attend_kernel,
        out_shape=jax.ShapeDtypeStruct(query_rows.shape, query_rows.dtype),
        in_specs=[pl.BlockSpec(memory_space=pltpu.SMEM)] + [vmem] * 7,
        out_specs=vmem,
    )(offset, query_rows, early_keys, late_keys, qpos, qdoc, kpos, kdoc)


def solution(mesh):
    placed = (P("seq", "ctx", None), P(None, "seq"), P("seq", None), P("seq", None))
    return jax.shard_map(
        body, mesh=mesh, in_specs=placed, out_specs=P("seq", "ctx", None), check_vma=False
    )
```

```python
import jax
import jax.numpy as jnp
from jax import lax
from jax.sharding import PartitionSpec as P
from jax.experimental import pallas as pl
from jax.experimental.pallas import tpu as pltpu

QUERY_HEADS = 16
KEY_VALUE_HEADS = 4
HEAD_SIZE = 64
QUERY_PER_KV = 4
SPAN = 64
DOC_MOST = 1024
WINDOW = DOC_MOST // SPAN


def apply_rotary(value_rows, token_positions):
    token_count = value_rows.shape[0]
    heads = value_rows.reshape(token_count, -1, HEAD_SIZE)
    half = HEAD_SIZE // 2
    freq = 500000.0 ** (-jnp.arange(half, dtype=jnp.float32) * 2.0 / HEAD_SIZE)
    angle = token_positions.astype(jnp.float32)[:, None] * freq[None, :]
    cosine = jnp.cos(angle)[:, None, :]
    sine = jnp.sin(angle)[:, None, :]
    first = heads[..., :half]
    second = heads[..., half:]
    turned = jnp.concatenate(
        [first * cosine - second * sine, second * cosine + first * sine], axis=-1
    )
    return turned.reshape(token_count, -1)


def positions(order_row):
    offsets = jnp.arange(SPAN, dtype=jnp.int32)
    return (order_row[:, None] * SPAN + offsets[None, :]).reshape(-1)


def documents(lengths_row, token_positions):
    ends = jnp.cumsum(lengths_row)
    return jnp.sum((ends[None, :] <= token_positions[..., None]).astype(jnp.int32), axis=-1)


def moved(value, count, pairs):
    pairs = [(s, d) for s, d in pairs if 0 <= s < count and 0 <= d < count]
    if not pairs:
        return jnp.zeros_like(value)
    return lax.ppermute(value, "ctx", pairs)


def chip_of(index, lanes):
    line, core = divmod(index // lanes, 2)
    half, rest = divmod(index % lanes, lanes // 2)
    return line, core, half, rest


def device_of(line, core, half, rest, lanes, lines):
    return (2 * line + core) * lanes + half * (lanes // 2) + rest


def project(rows, weight):
    lines = lax.axis_size("seq") // 2
    lanes = lax.axis_size("ctx")
    total = 2 * lines * lanes
    both = ("seq", "ctx")

    def pairs_for(offset):
        found = []
        for dest in range(total):
            line, core, half, rest = chip_of(dest, lanes)
            level = half * lines + line + offset(core)
            level %= 2 * lines
            found.append((device_of(level % lines, core, level // lines, rest, lanes, lines), dest))
        return found

    def mate_pairs():
        found = []
        for dest in range(total):
            line, core, half, rest = chip_of(dest, lanes)
            found.append((device_of(line, 1 - core, half, rest, lanes, lines), dest))
        return found

    step = [lambda core: 0]
    for shift in range(1, lines):
        if 2 * shift == lines:
            step.append(lambda core, s=shift: s if core == 0 else -s)
        elif 2 * shift < lines:
            step.append(lambda core, s=shift: s)
        else:
            step.append(lambda core, s=shift: s - lines)
    mine = [weight] + [lax.ppermute(weight, both, pairs_for(f)) for f in step[1:]]
    mate = lax.ppermute(jnp.stack(mine), both, mate_pairs())
    parts = [jnp.dot(rows, block, preferred_element_type=jnp.float32) for block in mine]
    parts += [
        jnp.dot(rows, mate[index], preferred_element_type=jnp.float32) for index in range(len(mine))
    ]
    parts = jnp.stack(parts).astype(jnp.bfloat16)
    seq_index = lax.axis_index("seq")
    line, core = seq_index // 2, seq_index % 2
    wanted = jnp.arange(2 * lines, dtype=jnp.int32)
    slot = (wanted // 2 - line) % lines + lines * (wanted % 2 != core).astype(jnp.int32)
    ordered = jnp.take(parts, slot, axis=0)
    return jnp.transpose(ordered, (1, 0, 2)).reshape(rows.shape[0], -1)


def body(tokens, qkv_weight, doc_lengths, span_order):
    rows = tokens[0]
    token_count = rows.shape[0]
    query_key_value = project(rows, qkv_weight)
    lengths_row = doc_lengths[0]
    order_row = span_order[0]
    places_all = positions(order_row)
    my_index = lax.axis_index("ctx")
    devices = lax.axis_size("ctx")
    first_row = my_index * token_count
    token_positions = lax.dynamic_slice_in_dim(places_all, first_row, token_count)
    query_rows = apply_rotary(
        query_key_value[:, : QUERY_HEADS * HEAD_SIZE].astype(jnp.float32), token_positions
    ).astype(jnp.bfloat16)
    key_rows = apply_rotary(
        query_key_value[
            :, QUERY_HEADS * HEAD_SIZE : (QUERY_HEADS + KEY_VALUE_HEADS) * HEAD_SIZE
        ].astype(jnp.float32),
        token_positions,
    ).astype(jnp.bfloat16)
    value_rows = query_key_value[:, (QUERY_HEADS + KEY_VALUE_HEADS) * HEAD_SIZE :]
    key_cols = key_rows.shape[1]
    stacked = jnp.concatenate([key_rows, value_rows], axis=1)

    early_first = order_row[2 * my_index] < devices
    offset = jnp.where(early_first, 0, SPAN).astype(jnp.int32)
    early_rows = lax.dynamic_slice_in_dim(stacked, offset, SPAN, 0)
    late_rows = lax.dynamic_slice_in_dim(stacked, SPAN - offset, SPAN, 0)
    early_queries = lax.dynamic_slice_in_dim(query_rows, offset, SPAN, 0)
    late_queries = lax.dynamic_slice_in_dim(query_rows, SPAN - offset, SPAN, 0)

    count = devices
    radix = 4
    up = early_rows[None]
    down = jnp.stack([early_rows, late_rows])[None]
    tail = range(count - WINDOW // 2, count)
    reach = 1
    while reach < WINDOW:
        ups, downs = [up], [down]
        for times in range(1, radix):
            shift = reach * times
            ups.append(moved(up, count, [(d, d + shift) for d in range(count)]))
            if shift < WINDOW // 2:
                downs.append(moved(down, count, [(d, d - shift) for d in range(count)]))
            else:
                downs.append(
                    jnp.stack(
                        [
                            moved(down[:, 0], count, [(d, d - shift) for d in tail]),
                            moved(down[:, 1], count, [(d, d - shift) for d in range(count)]),
                        ],
                        axis=1,
                    )
                )
        up = jnp.concatenate(ups, axis=0)
        down = jnp.concatenate(downs, axis=0)
        reach *= radix
    up = jnp.concatenate(
        [up, moved(early_rows[None], count, [(d, d + WINDOW) for d in range(count)])], axis=0
    )
    far = moved(late_rows[None], count, [(d, d - WINDOW) for d in range(count)])
    down = jnp.concatenate([down, jnp.stack([jnp.zeros_like(far), far], axis=1)], axis=0)
    early_keys = up.reshape(-1, up.shape[-1])
    around = jnp.concatenate([up, down[:, 0], down[:, 1]], axis=0)
    steps = jnp.arange(WINDOW + 1, dtype=jnp.int32)
    source = 2 * count - 1 - my_index - steps
    pick = jnp.where(
        my_index + steps <= count - 1,
        2 * (WINDOW + 1) + steps,
        jnp.where(source <= my_index, my_index - source, WINDOW + 1 + source - my_index),
    )
    pick = jnp.clip(pick, 0, around.shape[0] - 1)
    late_keys = jnp.take(around, pick, axis=0).reshape(-1, up.shape[-1])
    key_blocks = jnp.stack([early_keys, late_keys])

    steps = jnp.arange(WINDOW + 1, dtype=jnp.int32)
    query_spans = jnp.stack([my_index, 2 * devices - 1 - my_index])
    key_spans = query_spans[:, None] - steps[None, :]
    ramp = jnp.arange(SPAN, dtype=jnp.int32)
    key_places = (key_spans[:, :, None] * SPAN + ramp).reshape(2, -1)
    key_ok = jnp.repeat(key_spans >= 0, SPAN, axis=1)
    query_places = query_spans[:, None] * SPAN + ramp[None, :]
    key_docs = documents(lengths_row, key_places)
    query_docs = documents(lengths_row, query_places)
    live = (
        (query_docs[:, :, None] == key_docs[:, None, :])
        & (key_places[:, None, :] <= query_places[:, :, None])
        & key_ok[:, None, :]
    )

    key_docs = jnp.where(key_ok, key_docs, -1)
    return attend(
        offset.reshape(1),
        query_rows,
        early_keys,
        late_keys,
        query_places[:, :, None],
        query_docs[:, :, None],
        key_places[:, None, :],
        key_docs[:, None, :],
    )[None]


def attend_kernel(offset_ref, q_ref, early_ref, late_ref, qpos_ref, qdoc_ref, kpos_ref, kdoc_ref, o_ref):
    offset = pl.multiple_of(offset_ref[0], SPAN)
    for span, kv_ref in ((0, early_ref), (1, late_ref)):
        row = offset if span == 0 else SPAN - offset
        row = pl.multiple_of(row, SPAN)
        live = (qdoc_ref[span] == kdoc_ref[span]) & (kpos_ref[span] <= qpos_ref[span])
        live = jnp.concatenate([live] * QUERY_PER_KV, axis=0)
        for group in range(KEY_VALUE_HEADS):
            key = kv_ref[:, group * HEAD_SIZE : (group + 1) * HEAD_SIZE]
            base = KEY_VALUE_HEADS * HEAD_SIZE + group * HEAD_SIZE
            value = kv_ref[:, base : base + HEAD_SIZE]
            heads = range(group * QUERY_PER_KV, (group + 1) * QUERY_PER_KV)
            query = jnp.concatenate(
                [q_ref[pl.ds(row, SPAN), head * HEAD_SIZE : (head + 1) * HEAD_SIZE] for head in heads],
                axis=0,
            )
            scores = lax.dot_general(
                query, key, (((1,), (1,)), ((), ())), preferred_element_type=jnp.float32
            ) * 0.125
            scores = jnp.where(live, scores, -1e30)
            top = jnp.max(scores, axis=1, keepdims=True)
            weights = jnp.exp(scores - top)
            total = jnp.sum(weights, axis=1, keepdims=True)
            summed = jnp.dot(weights.astype(jnp.bfloat16), value, preferred_element_type=jnp.float32)
            result = (summed / total).astype(o_ref.dtype)
            for member, head in enumerate(heads):
                o_ref[pl.ds(row, SPAN), head * HEAD_SIZE : (head + 1) * HEAD_SIZE] = result[
                    member * SPAN : (member + 1) * SPAN
                ]


def attend(offset, query_rows, early_keys, late_keys, qpos, qdoc, kpos, kdoc):
    vmem = pl.BlockSpec(memory_space=pltpu.VMEM)
    return pl.pallas_call(
        attend_kernel,
        out_shape=jax.ShapeDtypeStruct(query_rows.shape, query_rows.dtype),
        in_specs=[pl.BlockSpec(memory_space=pltpu.SMEM)] + [vmem] * 7,
        out_specs=vmem,
    )(offset, query_rows, early_keys, late_keys, qpos, qdoc, kpos, kdoc)


def solution(mesh):
    placed = (P("seq", "ctx", None), P(None, "seq"), P("seq", None), P("seq", None))
    return jax.shard_map(
        body, mesh=mesh, in_specs=placed, out_specs=P("seq", "ctx", None), check_vma=False
    )
```

```python
import jax
import jax.numpy as jnp
from jax import lax
from jax.sharding import PartitionSpec as P
from jax.experimental import pallas as pl
from jax.experimental.pallas import tpu as pltpu

QUERY_HEADS = 16
KEY_VALUE_HEADS = 4
HEAD_SIZE = 64
QUERY_PER_KV = 4
SPAN = 64
DOC_MOST = 1024
WINDOW = DOC_MOST // SPAN


def apply_rotary(value_rows, token_positions):
    token_count = value_rows.shape[0]
    heads = value_rows.reshape(token_count, -1, HEAD_SIZE)
    half = HEAD_SIZE // 2
    freq = 500000.0 ** (-jnp.arange(half, dtype=jnp.float32) * 2.0 / HEAD_SIZE)
    angle = token_positions.astype(jnp.float32)[:, None] * freq[None, :]
    cosine = jnp.cos(angle)[:, None, :]
    sine = jnp.sin(angle)[:, None, :]
    first = heads[..., :half]
    second = heads[..., half:]
    turned = jnp.concatenate(
        [first * cosine - second * sine, second * cosine + first * sine], axis=-1
    )
    return turned.reshape(token_count, -1)


def positions(order_row):
    offsets = jnp.arange(SPAN, dtype=jnp.int32)
    return (order_row[:, None] * SPAN + offsets[None, :]).reshape(-1)


def documents(lengths_row, token_positions):
    ends = jnp.cumsum(lengths_row)
    return jnp.sum((ends[None, :] <= token_positions[..., None]).astype(jnp.int32), axis=-1)


def moved(value, count, pairs):
    pairs = [(s, d) for s, d in pairs if 0 <= s < count and 0 <= d < count]
    if not pairs:
        return jnp.zeros_like(value)
    return lax.ppermute(value, "ctx", pairs)


def chip_of(index, lanes):
    line, core = divmod(index // lanes, 2)
    half, rest = divmod(index % lanes, lanes // 2)
    return line, core, half, rest


def device_of(line, core, half, rest, lanes, lines):
    return (2 * line + core) * lanes + half * (lanes // 2) + rest


def project(rows, weight):
    lines = lax.axis_size("seq") // 2
    lanes = lax.axis_size("ctx")
    total = 2 * lines * lanes
    both = ("seq", "ctx")

    def pairs_for(offset):
        found = []
        for dest in range(total):
            line, core, half, rest = chip_of(dest, lanes)
            level = half * lines + line + offset(core)
            level %= 2 * lines
            found.append((device_of(level % lines, core, level // lines, rest, lanes, lines), dest))
        return found

    def mate_pairs():
        found = []
        for dest in range(total):
            line, core, half, rest = chip_of(dest, lanes)
            found.append((device_of(line, 1 - core, half, rest, lanes, lines), dest))
        return found

    step = [lambda core: 0]
    for shift in range(1, lines):
        if 2 * shift == lines:
            step.append(lambda core, s=shift: s if core == 0 else -s)
        elif 2 * shift < lines:
            step.append(lambda core, s=shift: s)
        else:
            step.append(lambda core, s=shift: s - lines)
    partner = lax.ppermute(rows, both, mate_pairs())
    mine = jnp.stack([weight] + [lax.ppermute(weight, both, pairs_for(f)) for f in step[1:]])
    own = jnp.einsum("td,bdn->btn", rows, mine, preferred_element_type=jnp.float32)
    theirs = jnp.einsum("td,bdn->btn", partner, mine, preferred_element_type=jnp.float32)
    mate = lax.ppermute(theirs.astype(jnp.bfloat16), both, mate_pairs())
    parts = jnp.concatenate([own.astype(jnp.bfloat16), mate], axis=0)
    seq_index = lax.axis_index("seq")
    line, core = seq_index // 2, seq_index % 2
    wanted = jnp.arange(2 * lines, dtype=jnp.int32)
    slot = (wanted // 2 - line) % lines + lines * (wanted % 2 != core).astype(jnp.int32)
    ordered = jnp.take(parts, slot, axis=0)
    return jnp.transpose(ordered, (1, 0, 2)).reshape(rows.shape[0], -1)


def body(tokens, qkv_weight, doc_lengths, span_order):
    rows = tokens[0]
    token_count = rows.shape[0]
    query_key_value = project(rows, qkv_weight)
    lengths_row = doc_lengths[0]
    order_row = span_order[0]
    places_all = positions(order_row)
    my_index = lax.axis_index("ctx")
    devices = lax.axis_size("ctx")
    first_row = my_index * token_count
    token_positions = lax.dynamic_slice_in_dim(places_all, first_row, token_count)
    query_rows = apply_rotary(
        query_key_value[:, : QUERY_HEADS * HEAD_SIZE].astype(jnp.float32), token_positions
    ).astype(jnp.bfloat16)
    key_rows = apply_rotary(
        query_key_value[
            :, QUERY_HEADS * HEAD_SIZE : (QUERY_HEADS + KEY_VALUE_HEADS) * HEAD_SIZE
        ].astype(jnp.float32),
        token_positions,
    ).astype(jnp.bfloat16)
    value_rows = query_key_value[:, (QUERY_HEADS + KEY_VALUE_HEADS) * HEAD_SIZE :]
    key_cols = key_rows.shape[1]
    stacked = jnp.concatenate([key_rows, value_rows], axis=1)

    early_first = order_row[2 * my_index] < devices
    offset = jnp.where(early_first, 0, SPAN).astype(jnp.int32)
    early_rows = lax.dynamic_slice_in_dim(stacked, offset, SPAN, 0)
    late_rows = lax.dynamic_slice_in_dim(stacked, SPAN - offset, SPAN, 0)
    early_queries = lax.dynamic_slice_in_dim(query_rows, offset, SPAN, 0)
    late_queries = lax.dynamic_slice_in_dim(query_rows, SPAN - offset, SPAN, 0)

    count = devices
    up = early_rows[None]
    down = jnp.stack([early_rows, late_rows])[None]
    reach = 1
    while reach < WINDOW:
        up = jnp.concatenate(
            [up, moved(up, count, [(d, d + reach) for d in range(count)])], axis=0
        )
        if 2 * reach < WINDOW:
            got = moved(down, count, [(d, d - reach) for d in range(count)])
        else:
            tail = range(count - reach, count)
            got = jnp.stack(
                [
                    moved(down[:, 0], count, [(d, d - reach) for d in tail]),
                    moved(down[:, 1], count, [(d, d - reach) for d in range(count)]),
                ],
                axis=1,
            )
        down = jnp.concatenate([down, got], axis=0)
        reach *= 2
    up = jnp.concatenate(
        [up, moved(early_rows[None], count, [(d, d + WINDOW) for d in range(count)])], axis=0
    )
    far = moved(late_rows[None], count, [(d, d - WINDOW) for d in range(count)])
    down = jnp.concatenate([down, jnp.stack([jnp.zeros_like(far), far], axis=1)], axis=0)
    early_keys = up.reshape(-1, up.shape[-1])
    around = jnp.concatenate([up, down[:, 0], down[:, 1]], axis=0)
    steps = jnp.arange(WINDOW + 1, dtype=jnp.int32)
    source = 2 * count - 1 - my_index - steps
    pick = jnp.where(
        my_index + steps <= count - 1,
        2 * (WINDOW + 1) + steps,
        jnp.where(source <= my_index, my_index - source, WINDOW + 1 + source - my_index),
    )
    pick = jnp.clip(pick, 0, around.shape[0] - 1)
    late_keys = jnp.take(around, pick, axis=0).reshape(-1, up.shape[-1])
    key_blocks = jnp.stack([early_keys, late_keys])

    steps = jnp.arange(WINDOW + 1, dtype=jnp.int32)
    query_spans = jnp.stack([my_index, 2 * devices - 1 - my_index])
    key_spans = query_spans[:, None] - steps[None, :]
    ramp = jnp.arange(SPAN, dtype=jnp.int32)
    key_places = (key_spans[:, :, None] * SPAN + ramp).reshape(2, -1)
    key_ok = jnp.repeat(key_spans >= 0, SPAN, axis=1)
    query_places = query_spans[:, None] * SPAN + ramp[None, :]
    key_docs = documents(lengths_row, key_places)
    query_docs = documents(lengths_row, query_places)
    live = (
        (query_docs[:, :, None] == key_docs[:, None, :])
        & (key_places[:, None, :] <= query_places[:, :, None])
        & key_ok[:, None, :]
    )

    key_docs = jnp.where(key_ok, key_docs, -1)
    return attend(
        offset.reshape(1),
        query_rows,
        early_keys,
        late_keys,
        query_places[:, :, None],
        query_docs[:, :, None],
        key_places[:, None, :],
        key_docs[:, None, :],
    )[None]


def attend_kernel(offset_ref, q_ref, early_ref, late_ref, qpos_ref, qdoc_ref, kpos_ref, kdoc_ref, o_ref):
    offset = pl.multiple_of(offset_ref[0], SPAN)
    for span, kv_ref in ((0, early_ref), (1, late_ref)):
        row = offset if span == 0 else SPAN - offset
        row = pl.multiple_of(row, SPAN)
        live = (qdoc_ref[span] == kdoc_ref[span]) & (kpos_ref[span] <= qpos_ref[span])
        live = jnp.concatenate([live] * QUERY_PER_KV, axis=0)
        for group in range(KEY_VALUE_HEADS):
            key = kv_ref[:, group * HEAD_SIZE : (group + 1) * HEAD_SIZE]
            base = KEY_VALUE_HEADS * HEAD_SIZE + group * HEAD_SIZE
            value = kv_ref[:, base : base + HEAD_SIZE]
            heads = range(group * QUERY_PER_KV, (group + 1) * QUERY_PER_KV)
            query = jnp.concatenate(
                [q_ref[pl.ds(row, SPAN), head * HEAD_SIZE : (head + 1) * HEAD_SIZE] for head in heads],
                axis=0,
            )
            scores = lax.dot_general(
                query, key, (((1,), (1,)), ((), ())), preferred_element_type=jnp.float32
            ) * 0.125
            scores = jnp.where(live, scores, -1e30)
            top = jnp.max(scores, axis=1, keepdims=True)
            weights = jnp.exp(scores - top)
            total = jnp.sum(weights, axis=1, keepdims=True)
            summed = jnp.dot(weights.astype(jnp.bfloat16), value, preferred_element_type=jnp.float32)
            result = (summed / total).astype(o_ref.dtype)
            for member, head in enumerate(heads):
                o_ref[pl.ds(row, SPAN), head * HEAD_SIZE : (head + 1) * HEAD_SIZE] = result[
                    member * SPAN : (member + 1) * SPAN
                ]


def attend(offset, query_rows, early_keys, late_keys, qpos, qdoc, kpos, kdoc):
    vmem = pl.BlockSpec(memory_space=pltpu.VMEM)
    return pl.pallas_call(
        attend_kernel,
        out_shape=jax.ShapeDtypeStruct(query_rows.shape, query_rows.dtype),
        in_specs=[pl.BlockSpec(memory_space=pltpu.SMEM)] + [vmem] * 7,
        out_specs=vmem,
    )(offset, query_rows, early_keys, late_keys, qpos, qdoc, kpos, kdoc)


def solution(mesh):
    placed = (P("seq", "ctx", None), P(None, "seq"), P("seq", None), P("seq", None))
    return jax.shard_map(
        body, mesh=mesh, in_specs=placed, out_specs=P("seq", "ctx", None), check_vma=False
    )
```

```python
import jax
import jax.numpy as jnp
from jax import lax
from jax.sharding import PartitionSpec as P
from jax.experimental import pallas as pl
from jax.experimental.pallas import tpu as pltpu

QUERY_HEADS = 16
KEY_VALUE_HEADS = 4
HEAD_SIZE = 64
QUERY_PER_KV = 4
SPAN = 64
DOC_MOST = 1024
WINDOW = DOC_MOST // SPAN


def apply_rotary(value_rows, token_positions):
    token_count = value_rows.shape[0]
    heads = value_rows.reshape(token_count, -1, HEAD_SIZE)
    half = HEAD_SIZE // 2
    freq = 500000.0 ** (-jnp.arange(half, dtype=jnp.float32) * 2.0 / HEAD_SIZE)
    angle = token_positions.astype(jnp.float32)[:, None] * freq[None, :]
    cosine = jnp.cos(angle)[:, None, :]
    sine = jnp.sin(angle)[:, None, :]
    first = heads[..., :half]
    second = heads[..., half:]
    turned = jnp.concatenate(
        [first * cosine - second * sine, second * cosine + first * sine], axis=-1
    )
    return turned.reshape(token_count, -1)


def positions(order_row):
    offsets = jnp.arange(SPAN, dtype=jnp.int32)
    return (order_row[:, None] * SPAN + offsets[None, :]).reshape(-1)


def documents(lengths_row, token_positions):
    ends = jnp.cumsum(lengths_row)
    return jnp.sum((ends[None, :] <= token_positions[..., None]).astype(jnp.int32), axis=-1)


def moved(value, count, pairs):
    pairs = [(s, d) for s, d in pairs if 0 <= s < count and 0 <= d < count]
    if not pairs:
        return jnp.zeros_like(value)
    return lax.ppermute(value, "ctx", pairs)


def chip_of(index, lanes):
    line, core = divmod(index // lanes, 2)
    half, rest = divmod(index % lanes, lanes // 2)
    return line, core, half, rest


def device_of(line, core, half, rest, lanes, lines):
    return (2 * line + core) * lanes + half * (lanes // 2) + rest


def project(rows, weight):
    lines = lax.axis_size("seq") // 2
    lanes = lax.axis_size("ctx")
    total = 2 * lines * lanes
    both = ("seq", "ctx")

    def pairs_for(offset):
        found = []
        for dest in range(total):
            line, core, half, rest = chip_of(dest, lanes)
            level = half * lines + line + offset(core)
            level %= 2 * lines
            found.append((device_of(level % lines, core, level // lines, rest, lanes, lines), dest))
        return found

    def mate_pairs():
        found = []
        for dest in range(total):
            line, core, half, rest = chip_of(dest, lanes)
            found.append((device_of(line, 1 - core, half, rest, lanes, lines), dest))
        return found

    step = [lambda core: 0]
    for shift in range(1, lines):
        if 2 * shift == lines:
            step.append(lambda core, s=shift: s if core == 0 else -s)
        elif 2 * shift < lines:
            step.append(lambda core, s=shift: s)
        else:
            step.append(lambda core, s=shift: s - lines)
    partner = lax.ppermute(rows, both, mate_pairs())
    mine = jnp.stack([weight] + [lax.ppermute(weight, both, pairs_for(f)) for f in step[1:]])
    own = jnp.einsum("td,bdn->btn", rows, mine, preferred_element_type=jnp.float32)
    theirs = jnp.einsum("td,bdn->btn", partner, mine, preferred_element_type=jnp.float32)
    mate = lax.ppermute(theirs.astype(jnp.bfloat16), both, mate_pairs())
    parts = jnp.concatenate([own.astype(jnp.bfloat16), mate], axis=0)
    seq_index = lax.axis_index("seq")
    line, core = seq_index // 2, seq_index % 2
    wanted = jnp.arange(2 * lines, dtype=jnp.int32)
    slot = (wanted // 2 - line) % lines + lines * (wanted % 2 != core).astype(jnp.int32)
    ordered = jnp.take(parts, slot, axis=0)
    return jnp.transpose(ordered, (1, 0, 2)).reshape(rows.shape[0], -1)


def body(tokens, qkv_weight, doc_lengths, span_order):
    rows = tokens[0]
    token_count = rows.shape[0]
    query_key_value = project(rows, qkv_weight)
    lengths_row = doc_lengths[0]
    order_row = span_order[0]
    places_all = positions(order_row)
    my_index = lax.axis_index("ctx")
    devices = lax.axis_size("ctx")
    first_row = my_index * token_count
    token_positions = lax.dynamic_slice_in_dim(places_all, first_row, token_count)
    query_rows = apply_rotary(
        query_key_value[:, : QUERY_HEADS * HEAD_SIZE].astype(jnp.float32), token_positions
    ).astype(jnp.bfloat16)
    key_rows = apply_rotary(
        query_key_value[
            :, QUERY_HEADS * HEAD_SIZE : (QUERY_HEADS + KEY_VALUE_HEADS) * HEAD_SIZE
        ].astype(jnp.float32),
        token_positions,
    ).astype(jnp.bfloat16)
    value_rows = query_key_value[:, (QUERY_HEADS + KEY_VALUE_HEADS) * HEAD_SIZE :]
    key_cols = key_rows.shape[1]
    stacked = jnp.concatenate([key_rows, value_rows], axis=1)

    early_first = order_row[2 * my_index] < devices
    offset = jnp.where(early_first, 0, SPAN).astype(jnp.int32)
    early_rows = lax.dynamic_slice_in_dim(stacked, offset, SPAN, 0)
    late_rows = lax.dynamic_slice_in_dim(stacked, SPAN - offset, SPAN, 0)
    early_queries = lax.dynamic_slice_in_dim(query_rows, offset, SPAN, 0)
    late_queries = lax.dynamic_slice_in_dim(query_rows, SPAN - offset, SPAN, 0)

    count = devices
    up = early_rows[None]
    down = jnp.stack([early_rows, late_rows])[None]
    reach = 1
    while reach < WINDOW:
        up = jnp.concatenate(
            [up, moved(up, count, [(d, d + reach) for d in range(count)])], axis=0
        )
        if 2 * reach < WINDOW:
            got = moved(down, count, [(d, d - reach) for d in range(count)])
        else:
            tail = range(count - reach, count)
            got = jnp.stack(
                [
                    moved(down[:, 0], count, [(d, d - reach) for d in tail]),
                    moved(down[:, 1], count, [(d, d - reach) for d in range(count)]),
                ],
                axis=1,
            )
        down = jnp.concatenate([down, got], axis=0)
        reach *= 2
    up = jnp.concatenate(
        [up, moved(early_rows[None], count, [(d, d + WINDOW) for d in range(count)])], axis=0
    )
    far = moved(late_rows[None], count, [(d, d - WINDOW) for d in range(count)])
    down = jnp.concatenate([down, jnp.stack([jnp.zeros_like(far), far], axis=1)], axis=0)
    early_keys = up.reshape(-1, up.shape[-1])
    steps = jnp.arange(WINDOW + 1, dtype=jnp.int32)
    source = 2 * count - 1 - my_index - steps
    from_up = (my_index + steps > count - 1) & (source <= my_index)
    up_row = jnp.where(from_up, my_index - source, 0)
    down_block = jnp.where(my_index + steps <= count - 1, 2 * steps + 1, 2 * (source - my_index))
    down_row = jnp.where(from_up, 0, down_block)
    up_row = jnp.clip(up_row, 0, WINDOW) * SPAN
    down_row = jnp.clip(down_row, 0, 2 * WINDOW + 1) * SPAN
    down_keys = down.reshape(-1, down.shape[-1])

    steps = jnp.arange(WINDOW + 1, dtype=jnp.int32)
    query_spans = jnp.stack([my_index, 2 * devices - 1 - my_index])
    key_spans = query_spans[:, None] - steps[None, :]
    ramp = jnp.arange(SPAN, dtype=jnp.int32)
    key_places = (key_spans[:, :, None] * SPAN + ramp).reshape(2, -1)
    key_ok = jnp.repeat(key_spans >= 0, SPAN, axis=1)
    query_places = query_spans[:, None] * SPAN + ramp[None, :]
    key_docs = documents(lengths_row, key_places)
    query_docs = documents(lengths_row, query_places)
    live = (
        (query_docs[:, :, None] == key_docs[:, None, :])
        & (key_places[:, None, :] <= query_places[:, :, None])
        & key_ok[:, None, :]
    )

    key_docs = jnp.where(key_ok, key_docs, -1)
    meta = jnp.concatenate(
        [offset.reshape(1), from_up.astype(jnp.int32), up_row, down_row]
    ).astype(jnp.int32)
    return attend(
        meta,
        query_rows,
        early_keys,
        down_keys,
        query_places[:, :, None],
        query_docs[:, :, None],
        key_places[:, None, :],
        key_docs[:, None, :],
    )[None]


def attend_kernel(
    meta_ref, q_ref, early_ref, down_ref, qpos_ref, qdoc_ref, kpos_ref, kdoc_ref, o_ref, late_ref
):
    offset = pl.multiple_of(meta_ref[0], SPAN)
    blocks = WINDOW + 1
    for step in range(blocks):
        up_row = pl.multiple_of(meta_ref[1 + blocks + step], SPAN)
        down_row = pl.multiple_of(meta_ref[1 + 2 * blocks + step], SPAN)
        late_ref[step * SPAN : (step + 1) * SPAN, :] = jnp.where(
            meta_ref[1 + step] > 0,
            early_ref[pl.ds(up_row, SPAN), :],
            down_ref[pl.ds(down_row, SPAN), :],
        )
    for span, kv_ref in ((0, early_ref), (1, late_ref)):
        row = offset if span == 0 else SPAN - offset
        row = pl.multiple_of(row, SPAN)
        live = (qdoc_ref[span] == kdoc_ref[span]) & (kpos_ref[span] <= qpos_ref[span])
        live = jnp.concatenate([live] * QUERY_PER_KV, axis=0)
        for group in range(KEY_VALUE_HEADS):
            key = kv_ref[:, group * HEAD_SIZE : (group + 1) * HEAD_SIZE]
            base = KEY_VALUE_HEADS * HEAD_SIZE + group * HEAD_SIZE
            value = kv_ref[:, base : base + HEAD_SIZE]
            heads = range(group * QUERY_PER_KV, (group + 1) * QUERY_PER_KV)
            query = jnp.concatenate(
                [q_ref[pl.ds(row, SPAN), head * HEAD_SIZE : (head + 1) * HEAD_SIZE] for head in heads],
                axis=0,
            )
            scores = lax.dot_general(
                query, key, (((1,), (1,)), ((), ())), preferred_element_type=jnp.float32
            ) * 0.125
            scores = jnp.where(live, scores, -1e30)
            top = jnp.max(scores, axis=1, keepdims=True)
            weights = jnp.exp(scores - top)
            total = jnp.sum(weights, axis=1, keepdims=True)
            summed = jnp.dot(weights.astype(jnp.bfloat16), value, preferred_element_type=jnp.float32)
            result = (summed / total).astype(o_ref.dtype)
            for member, head in enumerate(heads):
                o_ref[pl.ds(row, SPAN), head * HEAD_SIZE : (head + 1) * HEAD_SIZE] = result[
                    member * SPAN : (member + 1) * SPAN
                ]


def attend(meta, query_rows, early_keys, down_keys, qpos, qdoc, kpos, kdoc):
    vmem = pl.BlockSpec(memory_space=pltpu.VMEM)
    return pl.pallas_call(
        attend_kernel,
        out_shape=jax.ShapeDtypeStruct(query_rows.shape, query_rows.dtype),
        in_specs=[pl.BlockSpec(memory_space=pltpu.SMEM)] + [vmem] * 7,
        out_specs=vmem,
        scratch_shapes=[pltpu.VMEM(early_keys.shape, early_keys.dtype)],
    )(meta, query_rows, early_keys, down_keys, qpos, qdoc, kpos, kdoc)

def solution(mesh):
    placed = (P("seq", "ctx", None), P(None, "seq"), P("seq", None), P("seq", None))
    return jax.shard_map(
        body, mesh=mesh, in_specs=placed, out_specs=P("seq", "ctx", None), check_vma=False
    )
```

```python
import jax
import jax.numpy as jnp
from jax import lax
from jax.sharding import PartitionSpec as P
from jax.experimental import pallas as pl
from jax.experimental.pallas import tpu as pltpu

QUERY_HEADS = 16
KEY_VALUE_HEADS = 4
HEAD_SIZE = 64
QUERY_PER_KV = 4
SPAN = 64
DOC_MOST = 1024
WINDOW = DOC_MOST // SPAN


def apply_rotary(value_rows, token_positions):
    token_count = value_rows.shape[0]
    heads = value_rows.reshape(token_count, -1, HEAD_SIZE)
    half = HEAD_SIZE // 2
    freq = 500000.0 ** (-jnp.arange(half, dtype=jnp.float32) * 2.0 / HEAD_SIZE)
    angle = token_positions.astype(jnp.float32)[:, None] * freq[None, :]
    cosine = jnp.cos(angle)[:, None, :]
    sine = jnp.sin(angle)[:, None, :]
    first = heads[..., :half]
    second = heads[..., half:]
    turned = jnp.concatenate(
        [first * cosine - second * sine, second * cosine + first * sine], axis=-1
    )
    return turned.reshape(token_count, -1)


def positions(order_row):
    offsets = jnp.arange(SPAN, dtype=jnp.int32)
    return (order_row[:, None] * SPAN + offsets[None, :]).reshape(-1)


def documents(lengths_row, token_positions):
    ends = jnp.cumsum(lengths_row)
    return jnp.sum((ends[None, :] <= token_positions[..., None]).astype(jnp.int32), axis=-1)


def moved(value, count, pairs):
    pairs = [(s, d) for s, d in pairs if 0 <= s < count and 0 <= d < count]
    if not pairs:
        return jnp.zeros_like(value)
    return lax.ppermute(value, "ctx", pairs)


def chip_of(index, lanes):
    line, core = divmod(index // lanes, 2)
    half, rest = divmod(index % lanes, lanes // 2)
    return line, core, half, rest


def device_of(line, core, half, rest, lanes, lines):
    return (2 * line + core) * lanes + half * (lanes // 2) + rest


def project(rows, weight):
    lines = lax.axis_size("seq") // 2
    lanes = lax.axis_size("ctx")
    total = 2 * lines * lanes
    both = ("seq", "ctx")

    def pairs_for(offset):
        found = []
        for dest in range(total):
            line, core, half, rest = chip_of(dest, lanes)
            level = half * lines + line + offset(core)
            level %= 2 * lines
            found.append((device_of(level % lines, core, level // lines, rest, lanes, lines), dest))
        return found

    def mate_pairs():
        found = []
        for dest in range(total):
            line, core, half, rest = chip_of(dest, lanes)
            found.append((device_of(line, 1 - core, half, rest, lanes, lines), dest))
        return found

    step = [lambda core: 0]
    for shift in range(1, lines):
        if 2 * shift == lines:
            step.append(lambda core, s=shift: s if core == 0 else -s)
        elif 2 * shift < lines:
            step.append(lambda core, s=shift: s)
        else:
            step.append(lambda core, s=shift: s - lines)
    partner = lax.ppermute(rows, both, mate_pairs())
    mine = jnp.stack([weight] + [lax.ppermute(weight, both, pairs_for(f)) for f in step[1:]])
    own = jnp.einsum("td,bdn->btn", rows, mine, preferred_element_type=jnp.float32)
    theirs = jnp.einsum("td,bdn->btn", partner, mine, preferred_element_type=jnp.float32)
    mate = lax.ppermute(theirs.astype(jnp.bfloat16), both, mate_pairs())
    parts = jnp.concatenate([own.astype(jnp.bfloat16), mate], axis=0)
    seq_index = lax.axis_index("seq")
    line, core = seq_index // 2, seq_index % 2
    wanted = jnp.arange(2 * lines, dtype=jnp.int32)
    slot = (wanted // 2 - line) % lines + lines * (wanted % 2 != core).astype(jnp.int32)
    ordered = jnp.take(parts, slot, axis=0)
    return jnp.transpose(ordered, (1, 0, 2)).reshape(rows.shape[0], -1)


def tip_pairs(count, half, base):
    window = 2 * half
    wanted = {}
    for dest in range(count - window, count - half):
        wanted[dest] = set(range(max(2 * count - 1 - window - dest, dest + half), count))
    pairs, used = [], set()
    for dest in sorted(wanted, key=lambda d: -len(wanted[d])):
        for src in range(count - half, count):
            held = set(range(src, count))
            if src not in used and wanted[dest] <= held and wanted[dest] <= set(range(base, count)):
                pairs.append((src, dest))
                used.add(src)
                break
        else:
            raise ValueError("no source")
    return pairs


def body(tokens, qkv_weight, doc_lengths, span_order):
    rows = tokens[0]
    token_count = rows.shape[0]
    query_key_value = project(rows, qkv_weight)
    lengths_row = doc_lengths[0]
    order_row = span_order[0]
    places_all = positions(order_row)
    my_index = lax.axis_index("ctx")
    devices = lax.axis_size("ctx")
    first_row = my_index * token_count
    token_positions = lax.dynamic_slice_in_dim(places_all, first_row, token_count)
    query_rows = apply_rotary(
        query_key_value[:, : QUERY_HEADS * HEAD_SIZE].astype(jnp.float32), token_positions
    ).astype(jnp.bfloat16)
    key_rows = apply_rotary(
        query_key_value[
            :, QUERY_HEADS * HEAD_SIZE : (QUERY_HEADS + KEY_VALUE_HEADS) * HEAD_SIZE
        ].astype(jnp.float32),
        token_positions,
    ).astype(jnp.bfloat16)
    value_rows = query_key_value[:, (QUERY_HEADS + KEY_VALUE_HEADS) * HEAD_SIZE :]
    key_cols = key_rows.shape[1]
    stacked = jnp.concatenate([key_rows, value_rows], axis=1)

    early_first = order_row[2 * my_index] < devices
    offset = jnp.where(early_first, 0, SPAN).astype(jnp.int32)
    early_rows = lax.dynamic_slice_in_dim(stacked, offset, SPAN, 0)
    late_rows = lax.dynamic_slice_in_dim(stacked, SPAN - offset, SPAN, 0)
    early_queries = lax.dynamic_slice_in_dim(query_rows, offset, SPAN, 0)
    late_queries = lax.dynamic_slice_in_dim(query_rows, SPAN - offset, SPAN, 0)

    count = devices
    half = WINDOW // 2
    base = count - half // 2
    up = early_rows[None]
    down = jnp.stack([early_rows, late_rows])[None]
    reach = 1
    while reach < WINDOW:
        up = jnp.concatenate(
            [up, moved(up, count, [(d, d + reach) for d in range(count)])], axis=0
        )
        if 2 * reach < WINDOW:
            got = moved(down, count, [(d, d - reach) for d in range(count)])
        else:
            padded = jnp.concatenate([jnp.zeros_like(down[: count - base, 0]), down[:, 0]], axis=0)
            start = jnp.clip(count - my_index, 0, padded.shape[0] - (count - base))
            tail_rows = lax.dynamic_slice_in_dim(padded, start, count - base, 0)
            tip = moved(tail_rows, count, tip_pairs(count, half, base))
            late = moved(down[:, 1], count, [(d, d - reach) for d in range(count)])
            got = jnp.stack([jnp.zeros_like(late), late], axis=1)
        down = jnp.concatenate([down, got], axis=0)
        reach *= 2
    up = jnp.concatenate(
        [up, moved(early_rows[None], count, [(d, d + WINDOW) for d in range(count)])], axis=0
    )
    far = moved(late_rows[None], count, [(d, d - WINDOW) for d in range(count)])
    down = jnp.concatenate([down, jnp.stack([jnp.zeros_like(far), far], axis=1)], axis=0)
    early_keys = up.reshape(-1, up.shape[-1])
    steps = jnp.arange(WINDOW + 1, dtype=jnp.int32)
    source = 2 * count - 1 - my_index - steps
    own_late = my_index + steps <= count - 1
    from_up = ~own_late & (source <= my_index)
    from_tip = ~own_late & (source - my_index >= half)
    kind = jnp.where(from_up, 1, jnp.where(from_tip, 2, 0)).astype(jnp.int32)
    up_row = jnp.clip(jnp.where(from_up, my_index - source, 0), 0, WINDOW) * SPAN
    down_block = jnp.where(own_late, 2 * steps + 1, 2 * (source - my_index))
    down_row = jnp.clip(jnp.where(from_up | from_tip, 0, down_block), 0, 2 * WINDOW + 1) * SPAN
    tip_row = jnp.clip(jnp.where(from_tip, source - base, 0), 0, count - base - 1) * SPAN
    down_keys = down.reshape(-1, down.shape[-1])
    tip_keys = tip.reshape(-1, tip.shape[-1])

    steps = jnp.arange(WINDOW + 1, dtype=jnp.int32)
    query_spans = jnp.stack([my_index, 2 * devices - 1 - my_index])
    key_spans = query_spans[:, None] - steps[None, :]
    ramp = jnp.arange(SPAN, dtype=jnp.int32)
    key_places = (key_spans[:, :, None] * SPAN + ramp).reshape(2, -1)
    key_ok = jnp.repeat(key_spans >= 0, SPAN, axis=1)
    query_places = query_spans[:, None] * SPAN + ramp[None, :]
    key_docs = documents(lengths_row, key_places)
    query_docs = documents(lengths_row, query_places)
    live = (
        (query_docs[:, :, None] == key_docs[:, None, :])
        & (key_places[:, None, :] <= query_places[:, :, None])
        & key_ok[:, None, :]
    )

    key_docs = jnp.where(key_ok, key_docs, -1)
    meta = jnp.concatenate(
        [offset.reshape(1), kind, up_row, down_row, tip_row]
    ).astype(jnp.int32)
    return attend(
        meta,
        query_rows,
        early_keys,
        down_keys,
        tip_keys,
        query_places[:, :, None],
        query_docs[:, :, None],
        key_places[:, None, :],
        key_docs[:, None, :],
    )[None]


def attend_kernel(
    meta_ref, q_ref, early_ref, down_ref, tip_ref, qpos_ref, qdoc_ref, kpos_ref, kdoc_ref, o_ref, late_ref
):
    offset = pl.multiple_of(meta_ref[0], SPAN)
    blocks = WINDOW + 1
    for step in range(blocks):
        kind = meta_ref[1 + step]
        up_row = pl.multiple_of(meta_ref[1 + blocks + step], SPAN)
        down_row = pl.multiple_of(meta_ref[1 + 2 * blocks + step], SPAN)
        tip_row = pl.multiple_of(meta_ref[1 + 3 * blocks + step], SPAN)
        late_ref[step * SPAN : (step + 1) * SPAN, :] = jnp.where(
            kind == 1,
            early_ref[pl.ds(up_row, SPAN), :],
            jnp.where(kind == 2, tip_ref[pl.ds(tip_row, SPAN), :], down_ref[pl.ds(down_row, SPAN), :]),
        )
    for span, kv_ref in ((0, early_ref), (1, late_ref)):
        row = offset if span == 0 else SPAN - offset
        row = pl.multiple_of(row, SPAN)
        live = (qdoc_ref[span] == kdoc_ref[span]) & (kpos_ref[span] <= qpos_ref[span])
        live = jnp.concatenate([live] * QUERY_PER_KV, axis=0)
        for group in range(KEY_VALUE_HEADS):
            key = kv_ref[:, group * HEAD_SIZE : (group + 1) * HEAD_SIZE]
            base = KEY_VALUE_HEADS * HEAD_SIZE + group * HEAD_SIZE
            value = kv_ref[:, base : base + HEAD_SIZE]
            heads = range(group * QUERY_PER_KV, (group + 1) * QUERY_PER_KV)
            query = jnp.concatenate(
                [q_ref[pl.ds(row, SPAN), head * HEAD_SIZE : (head + 1) * HEAD_SIZE] for head in heads],
                axis=0,
            )
            scores = lax.dot_general(
                query, key, (((1,), (1,)), ((), ())), preferred_element_type=jnp.float32
            ) * 0.125
            scores = jnp.where(live, scores, -1e30)
            top = jnp.max(scores, axis=1, keepdims=True)
            weights = jnp.exp(scores - top)
            total = jnp.sum(weights, axis=1, keepdims=True)
            summed = jnp.dot(weights.astype(jnp.bfloat16), value, preferred_element_type=jnp.float32)
            result = (summed / total).astype(o_ref.dtype)
            for member, head in enumerate(heads):
                o_ref[pl.ds(row, SPAN), head * HEAD_SIZE : (head + 1) * HEAD_SIZE] = result[
                    member * SPAN : (member + 1) * SPAN
                ]


def attend(meta, query_rows, early_keys, down_keys, tip_keys, qpos, qdoc, kpos, kdoc):
    vmem = pl.BlockSpec(memory_space=pltpu.VMEM)
    return pl.pallas_call(
        attend_kernel,
        out_shape=jax.ShapeDtypeStruct(query_rows.shape, query_rows.dtype),
        in_specs=[pl.BlockSpec(memory_space=pltpu.SMEM)] + [vmem] * 8,
        out_specs=vmem,
        scratch_shapes=[pltpu.VMEM(early_keys.shape, early_keys.dtype)],
    )(meta, query_rows, early_keys, down_keys, tip_keys, qpos, qdoc, kpos, kdoc)

def solution(mesh):
    placed = (P("seq", "ctx", None), P(None, "seq"), P("seq", None), P("seq", None))
    return jax.shard_map(
        body, mesh=mesh, in_specs=placed, out_specs=P("seq", "ctx", None), check_vma=False
    )
```

```python
import jax
import jax.numpy as jnp
from jax import lax
from jax.sharding import PartitionSpec as P
from jax.experimental import pallas as pl
from jax.experimental.pallas import tpu as pltpu

QUERY_HEADS = 16
KEY_VALUE_HEADS = 4
HEAD_SIZE = 64
QUERY_PER_KV = 4
SPAN = 64
DOC_MOST = 1024
WINDOW = DOC_MOST // SPAN


def apply_rotary(value_rows, token_positions):
    token_count = value_rows.shape[0]
    heads = value_rows.reshape(token_count, -1, HEAD_SIZE)
    half = HEAD_SIZE // 2
    freq = 500000.0 ** (-jnp.arange(half, dtype=jnp.float32) * 2.0 / HEAD_SIZE)
    angle = token_positions.astype(jnp.float32)[:, None] * freq[None, :]
    cosine = jnp.cos(angle)[:, None, :]
    sine = jnp.sin(angle)[:, None, :]
    first = heads[..., :half]
    second = heads[..., half:]
    turned = jnp.concatenate(
        [first * cosine - second * sine, second * cosine + first * sine], axis=-1
    )
    return turned.reshape(token_count, -1)


def positions(order_row):
    offsets = jnp.arange(SPAN, dtype=jnp.int32)
    return (order_row[:, None] * SPAN + offsets[None, :]).reshape(-1)


def documents(lengths_row, token_positions):
    ends = jnp.cumsum(lengths_row)
    return jnp.sum((ends[None, :] <= token_positions[..., None]).astype(jnp.int32), axis=-1)


def moved(value, count, pairs):
    pairs = [(s, d) for s, d in pairs if 0 <= s < count and 0 <= d < count]
    if not pairs:
        return jnp.zeros_like(value)
    return lax.ppermute(value, "ctx", pairs)


def chip_of(index, lanes):
    line, core = divmod(index // lanes, 2)
    half, rest = divmod(index % lanes, lanes // 2)
    return line, core, half, rest


def device_of(line, core, half, rest, lanes):
    return (2 * line + core) * lanes + half * (lanes // 2) + rest


def project(rows, weight):
    lines = lax.axis_size("seq") // 2
    lanes = lax.axis_size("ctx")
    total = 2 * lines * lanes
    both = ("seq", "ctx")

    def pairs_for(offset):
        found = []
        for dest in range(total):
            line, core, half, rest = chip_of(dest, lanes)
            level = half * lines + line + offset(core)
            level %= 2 * lines
            found.append((device_of(level % lines, core, level // lines, rest, lanes), dest))
        return found

    def mate_pairs():
        found = []
        for dest in range(total):
            line, core, half, rest = chip_of(dest, lanes)
            found.append((device_of(line, 1 - core, half, rest, lanes), dest))
        return found

    step = [lambda core: 0]
    for shift in range(1, lines):
        if 2 * shift == lines:
            step.append(lambda core, s=shift: s if core == 0 else -s)
        elif 2 * shift < lines:
            step.append(lambda core, s=shift: s)
        else:
            step.append(lambda core, s=shift: s - lines)
    partner = lax.ppermute(rows, both, mate_pairs())
    mine = jnp.stack([weight] + [lax.ppermute(weight, both, pairs_for(f)) for f in step[1:]])
    own = jnp.einsum("td,bdn->btn", rows, mine, preferred_element_type=jnp.float32)
    theirs = jnp.einsum("td,bdn->btn", partner, mine, preferred_element_type=jnp.float32)
    mate = lax.ppermute(theirs.astype(jnp.bfloat16), both, mate_pairs())
    parts = jnp.concatenate([own.astype(jnp.bfloat16), mate], axis=0)
    seq_index = lax.axis_index("seq")
    line, core = seq_index // 2, seq_index % 2
    wanted = jnp.arange(2 * lines, dtype=jnp.int32)
    slot = (wanted // 2 - line) % lines + lines * (wanted % 2 != core).astype(jnp.int32)
    ordered = jnp.take(parts, slot, axis=0)
    return jnp.transpose(ordered, (1, 0, 2)).reshape(rows.shape[0], -1)


def tip_pairs(count, half, base):
    window = 2 * half
    wanted = {}
    for dest in range(count - window, count - half):
        wanted[dest] = set(range(max(2 * count - 1 - window - dest, dest + half), count))
    pairs, used = [], set()
    for dest in sorted(wanted, key=lambda d: -len(wanted[d])):
        for src in range(count - half, count):
            held = set(range(src, count))
            if src not in used and wanted[dest] <= held and wanted[dest] <= set(range(base, count)):
                pairs.append((src, dest))
                used.add(src)
                break
        else:
            raise ValueError("no source")
    return pairs


def body(tokens, qkv_weight, doc_lengths, span_order):
    rows = tokens[0]
    token_count = rows.shape[0]
    query_key_value = project(rows, qkv_weight)
    lengths_row = doc_lengths[0]
    order_row = span_order[0]
    places_all = positions(order_row)
    my_index = lax.axis_index("ctx")
    devices = lax.axis_size("ctx")
    first_row = my_index * token_count
    token_positions = lax.dynamic_slice_in_dim(places_all, first_row, token_count)
    query_rows = apply_rotary(
        query_key_value[:, : QUERY_HEADS * HEAD_SIZE].astype(jnp.float32), token_positions
    ).astype(jnp.bfloat16)
    key_rows = apply_rotary(
        query_key_value[
            :, QUERY_HEADS * HEAD_SIZE : (QUERY_HEADS + KEY_VALUE_HEADS) * HEAD_SIZE
        ].astype(jnp.float32),
        token_positions,
    ).astype(jnp.bfloat16)
    value_rows = query_key_value[:, (QUERY_HEADS + KEY_VALUE_HEADS) * HEAD_SIZE :]
    stacked = jnp.concatenate([key_rows, value_rows], axis=1)

    early_first = order_row[2 * my_index] < devices
    offset = jnp.where(early_first, 0, SPAN).astype(jnp.int32)
    early_rows = lax.dynamic_slice_in_dim(stacked, offset, SPAN, 0)
    late_rows = lax.dynamic_slice_in_dim(stacked, SPAN - offset, SPAN, 0)
    early_queries = lax.dynamic_slice_in_dim(query_rows, offset, SPAN, 0)
    late_queries = lax.dynamic_slice_in_dim(query_rows, SPAN - offset, SPAN, 0)

    count = devices
    half = WINDOW // 2
    base = count - half // 2
    up = early_rows[None]
    down = jnp.stack([early_rows, late_rows])[None]
    reach = 1
    while reach < WINDOW:
        up = jnp.concatenate([up, moved(up, count, [(d, d + reach) for d in range(count)])], axis=0)
        if 2 * reach < WINDOW:
            got = moved(down, count, [(d, d - reach) for d in range(count)])
        else:
            padded = jnp.concatenate([jnp.zeros_like(down[: count - base, 0]), down[:, 0]], axis=0)
            start = jnp.clip(count - my_index, 0, padded.shape[0] - (count - base))
            tail_rows = lax.dynamic_slice_in_dim(padded, start, count - base, 0)
            tip = moved(tail_rows, count, tip_pairs(count, half, base))
            late = moved(down[:, 1], count, [(d, d - reach) for d in range(count)])
            got = jnp.stack([jnp.zeros_like(late), late], axis=1)
        down = jnp.concatenate([down, got], axis=0)
        reach *= 2
    up = jnp.concatenate(
        [up, moved(early_rows[None], count, [(d, d + WINDOW) for d in range(count)])], axis=0
    )
    far = moved(late_rows[None], count, [(d, d - WINDOW) for d in range(count)])
    down = jnp.concatenate([down, jnp.stack([jnp.zeros_like(far), far], axis=1)], axis=0)
    early_keys = up.reshape(-1, up.shape[-1])
    steps = jnp.arange(WINDOW + 1, dtype=jnp.int32)
    source = 2 * count - 1 - my_index - steps
    own_late = my_index + steps <= count - 1
    from_up = ~own_late & (source <= my_index)
    from_tip = ~own_late & (source - my_index >= half)
    kind = jnp.where(from_up, 1, jnp.where(from_tip, 2, 0)).astype(jnp.int32)
    up_row = jnp.clip(jnp.where(from_up, my_index - source, 0), 0, WINDOW) * SPAN
    down_block = jnp.where(own_late, 2 * steps + 1, 2 * (source - my_index))
    down_row = jnp.clip(jnp.where(from_up | from_tip, 0, down_block), 0, 2 * WINDOW + 1) * SPAN
    tip_row = jnp.clip(jnp.where(from_tip, source - base, 0), 0, count - base - 1) * SPAN
    down_keys = down.reshape(-1, down.shape[-1])
    tip_keys = tip.reshape(-1, tip.shape[-1])

    steps = jnp.arange(WINDOW + 1, dtype=jnp.int32)
    query_spans = jnp.stack([my_index, 2 * devices - 1 - my_index])
    key_spans = query_spans[:, None] - steps[None, :]
    ramp = jnp.arange(SPAN, dtype=jnp.int32)
    key_places = (key_spans[:, :, None] * SPAN + ramp).reshape(2, -1)
    key_ok = jnp.repeat(key_spans >= 0, SPAN, axis=1)
    query_places = query_spans[:, None] * SPAN + ramp[None, :]
    key_docs = documents(lengths_row, key_places)
    query_docs = documents(lengths_row, query_places)

    key_docs = jnp.where(key_ok, key_docs, -1)
    meta = jnp.concatenate(
        [offset.reshape(1), kind, up_row, down_row, tip_row]
    ).astype(jnp.int32)
    return attend(
        meta,
        query_rows,
        early_keys,
        down_keys,
        tip_keys,
        query_places[:, :, None],
        query_docs[:, :, None],
        key_places[:, None, :],
        key_docs[:, None, :],
    )[None]


def attend_kernel(
    meta_ref, q_ref, early_ref, down_ref, tip_ref, qpos_ref, qdoc_ref, kpos_ref, kdoc_ref, o_ref, late_ref
):
    offset = pl.multiple_of(meta_ref[0], SPAN)
    blocks = WINDOW + 1
    for step in range(blocks):
        kind = meta_ref[1 + step]
        up_row = pl.multiple_of(meta_ref[1 + blocks + step], SPAN)
        down_row = pl.multiple_of(meta_ref[1 + 2 * blocks + step], SPAN)
        tip_row = pl.multiple_of(meta_ref[1 + 3 * blocks + step], SPAN)
        late_ref[step * SPAN : (step + 1) * SPAN, :] = jnp.where(
            kind == 1,
            early_ref[pl.ds(up_row, SPAN), :],
            jnp.where(kind == 2, tip_ref[pl.ds(tip_row, SPAN), :], down_ref[pl.ds(down_row, SPAN), :]),
        )
    for span, kv_ref in ((0, early_ref), (1, late_ref)):
        row = offset if span == 0 else SPAN - offset
        row = pl.multiple_of(row, SPAN)
        live = (qdoc_ref[span] == kdoc_ref[span]) & (kpos_ref[span] <= qpos_ref[span])
        live = jnp.concatenate([live] * QUERY_PER_KV, axis=0)
        for group in range(KEY_VALUE_HEADS):
            key = kv_ref[:, group * HEAD_SIZE : (group + 1) * HEAD_SIZE]
            base = KEY_VALUE_HEADS * HEAD_SIZE + group * HEAD_SIZE
            value = kv_ref[:, base : base + HEAD_SIZE]
            heads = range(group * QUERY_PER_KV, (group + 1) * QUERY_PER_KV)
            query = jnp.concatenate(
                [q_ref[pl.ds(row, SPAN), head * HEAD_SIZE : (head + 1) * HEAD_SIZE] for head in heads],
                axis=0,
            )
            scores = lax.dot_general(
                query, key, (((1,), (1,)), ((), ())), preferred_element_type=jnp.float32
            ) * 0.125
            scores = jnp.where(live, scores, -1e30)
            top = jnp.max(scores, axis=1, keepdims=True)
            weights = jnp.exp(scores - top)
            total = jnp.sum(weights, axis=1, keepdims=True)
            summed = jnp.dot(weights.astype(jnp.bfloat16), value, preferred_element_type=jnp.float32)
            result = (summed / total).astype(o_ref.dtype)
            for member, head in enumerate(heads):
                o_ref[pl.ds(row, SPAN), head * HEAD_SIZE : (head + 1) * HEAD_SIZE] = result[
                    member * SPAN : (member + 1) * SPAN
                ]


def attend(meta, query_rows, early_keys, down_keys, tip_keys, qpos, qdoc, kpos, kdoc):
    vmem = pl.BlockSpec(memory_space=pltpu.VMEM)
    return pl.pallas_call(
        attend_kernel,
        out_shape=jax.ShapeDtypeStruct(query_rows.shape, query_rows.dtype),
        in_specs=[pl.BlockSpec(memory_space=pltpu.SMEM)] + [vmem] * 8,
        out_specs=vmem,
        scratch_shapes=[pltpu.VMEM(early_keys.shape, early_keys.dtype)],
    )(meta, query_rows, early_keys, down_keys, tip_keys, qpos, qdoc, kpos, kdoc)


def solution(mesh):
    placed = (P("seq", "ctx", None), P(None, "seq"), P("seq", None), P("seq", None))
    return jax.shard_map(
        body, mesh=mesh, in_specs=placed, out_specs=P("seq", "ctx", None), check_vma=False
    )
```
